256 devices in a mesh: ens: 4 (over z_hi), lon: 64 (over y, z_lo, x, core).
Axes of the slice: x: 4, y: 4, z: 8 (z_hi: 4, z_lo: 2; z = z_hi * 2 + z_lo), core: 2. Of those that a mesh axis runs over, the one named last changes fastest.
Arguments:
- tokens: bfloat16 [4, 2, 90, 128, 768], P('ens', None, None, 'lon'), may hold values from -6 to 6
- cotangent: bfloat16 [4, 2, 90, 128, 768], P('ens', None, None, 'lon'), may hold values from -6 to 6
- gain: float32 [768], replicated, may hold values from 0.1 to 1.9
- weight_one: bfloat16 [2, 8, 96, 96], replicated, may hold values from -0.4375 to 0.4375
- weight_two: bfloat16 [2, 8, 96, 96], replicated, may hold values from -0.4375 to 0.4375
- bias_one: float32 [2, 768], replicated, may hold values from -4 to 4
- bias_two: float32 [2, 768], replicated, may hold values from -4 to 4
Outputs:
- mixed: bfloat16 [4, 2, 90, 128, 768], P('ens', None, None, 'lon')
- grad_input: bfloat16 [4, 2, 90, 128, 768], P('ens', None, None, 'lon')
- grad_one: float32 [2, 8, 96, 96], P(None, 'ens')
- grad_two: float32 [2, 8, 96, 96], P(None, 'ens')
- grad_gain: float32 [768], P('ens')
The draws below stay inside these ranges and needn't reach their ends.
All inputs are finite; a program needn't handle non-finite values.
Results may differ from the reference program's by a relative error of at most 0.024.
Values may be sent and summed in bfloat16 or wider, within the bound.
No kernel may reach another device: no remote copies, remote signals or barrier semaphores. Data moves between devices by JAX's collectives and lax.ppermute only.
A program may use at most 64 MiB of HBM per device.

```python
import math
import jax
import jax.numpy as jnp
from jax import lax

C = 768
NBLOCK = 8
H = 90
SAMP = 2
BS = 96
MEMBERS = 4
W = 128


def raised(entries, key, source, target, parts, factor):
    owner, partner = [(jnp.arange(entries.shape[position]) // (entries.shape[position] // parts)).reshape([-1 if axis == position else 1 for axis in range(entries.ndim)]) for position in (source, target)]
    chosen = jax.random.permutation(key, parts)[partner]
    strong = (owner == chosen) | (owner == (partner + parts // 2) % parts)
    return jnp.where(strong, factor * entries, entries)


def steps_of(own_key, dims, cuts, smallest, top_value):
    def one(axis_at, parts):
        steps = jax.random.uniform(jax.random.fold_in(jax.random.fold_in(own_key, 6), axis_at), (parts,), jnp.float32, smallest / len(cuts), top_value / len(cuts))
        return jnp.repeat(jnp.exp(steps), dims[axis_at] // parts).reshape((-1,) + (1,) * (len(dims) - axis_at - 1))

    level = one(*cuts[0])
    for cut in cuts[1:]:
        level = level * one(*cut)
    return level


def scatter_about(stream_key, extent, deviation, most, cuts=(), held_as=jnp.bfloat16):
    result = deviation * jax.random.normal(stream_key, extent, jnp.float32)
    if cuts:
        result = result * steps_of(stream_key, extent, cuts, -0.22, 0.18)
    return jnp.clip(result, -most, most).astype(held_as)


def heavy_noise(own_key, shape, scale, reach, cuts, heavy, held_as=jnp.bfloat16):
    drawn = scale * jax.random.normal(own_key, shape, jnp.float32)
    if cuts:
        drawn = drawn * steps_of(own_key, shape, cuts, -0.22, 0.18)
    return jnp.clip(raised(drawn, jax.random.fold_in(own_key, 3), *heavy), -reach, reach).astype(held_as)


def setup_inputs(seed: int = 0) -> dict:
    key_of = jax.random.split(jax.random.key(seed), 8)
    return {
        "tokens": scatter_about(key_of[0], (MEMBERS, SAMP, H, W, C), 1.0, 6.0, ((0, 4), (3, 64))),
        "cotangent": heavy_noise(key_of[1], (MEMBERS, SAMP, H, W, C), 1.0, 6.0, ((0, 4), (3, 64)), (0, 4, 4, 2.0)),
        "gain": jnp.clip(1.0 + 0.18 * jax.random.normal(key_of[2], (C,), jnp.float32), 0.1, 1.9),
        "weight_one": scatter_about(key_of[3], (2, NBLOCK, BS, BS), (2 * BS) ** -0.5, 0.4375),
        "weight_two": scatter_about(key_of[4], (2, NBLOCK, BS, BS), (2 * BS) ** -0.5, 0.4375),
        "bias_one": scatter_about(key_of[5], (2, C), 1.0, 4.0, (), jnp.float32),
        "bias_two": scatter_about(key_of[6], (2, C), 1.0, 4.0, (), jnp.float32),
    }


eps_norm = 1e-05
gelu_coef = 0.044715

def rounded(value):
    return lax.optimization_barrier(value.astype(jnp.bfloat16))

def gelu_value(value):
    factor = math.sqrt(2.0 / math.pi)
    return 0.5 * value * (1.0 + jnp.tanh(factor * (value + gelu_coef * value * value * value)))

def gelu_slope(value):
    factor = math.sqrt(2.0 / math.pi)
    tangent = jnp.tanh(factor * (value + gelu_coef * value * value * value))
    return 0.5 * (1.0 + tangent) + 0.5 * value * (1.0 - tangent * tangent) * factor * (1.0 + 3.0 * gelu_coef * value * value)

def block_product(rows, weight):
    return jnp.einsum('rbj,bjk->rbk', rows.astype(jnp.float32), weight.astype(jnp.float32))

def block_adjoint(rows, weight):
    return jnp.einsum('rbk,bjk->rbj', rows.astype(jnp.float32), weight.astype(jnp.float32))

def block_outer(left, right):
    return jnp.einsum('rbj,rbk->bjk', left.astype(jnp.float32), right.astype(jnp.float32))

def reference(tokens, cotangent, gain, weight_one, weight_two, bias_one, bias_two):
    members, samples, latitudes, longitudes, width = tokens.shape
    blocks = weight_one.shape[1]
    block_size = weight_one.shape[2]
    modes = longitudes // 2
    scale = 1.0 / math.sqrt(latitudes * longitudes)
    mode_weights = jnp.where(jnp.arange(modes) == 0, 1.0, 2.0).astype(jnp.float32)
    bias_first = bias_one.astype(jnp.float32).reshape(2, blocks, block_size)
    bias_second = bias_two.astype(jnp.float32).reshape(2, blocks, block_size)

    def one_sample(pair):
        field, cot_field = pair
        values = field.astype(jnp.float32)
        center = values - lax.optimization_barrier(jnp.mean(values, axis=-1, keepdims=True))
        inv_dev = lax.rsqrt(lax.optimization_barrier(jnp.mean(center * center, axis=-1, keepdims=True)) + eps_norm)
        standard = center * inv_dev
        normed = rounded(standard * gain)
        lon_part = jnp.fft.rfft(normed.astype(jnp.float32), axis=1)[:, :modes]
        part_real = rounded(lon_part.real * scale)
        part_imag = rounded(lon_part.imag * scale)
        spectrum = jnp.fft.fft(part_real.astype(jnp.float32) + 1j * part_imag.astype(jnp.float32), axis=0)
        spec_real = rounded(spectrum.real).reshape(-1, blocks, block_size)
        spec_imag = rounded(spectrum.imag).reshape(-1, blocks, block_size)
        before_real = block_product(spec_real, weight_one[0]) - block_product(spec_imag, weight_one[1]) + bias_first[0]
        before_imag = block_product(spec_imag, weight_one[0]) + block_product(spec_real, weight_one[1]) + bias_first[1]
        hidden_real = rounded(gelu_value(before_real))
        hidden_imag = rounded(gelu_value(before_imag))
        filtered_real = rounded(block_product(hidden_real, weight_two[0]) - block_product(hidden_imag, weight_two[1]) + bias_second[0])
        filtered_imag = rounded(block_product(hidden_imag, weight_two[0]) + block_product(hidden_real, weight_two[1]) + bias_second[1])
        filtered = (filtered_real.astype(jnp.float32) + 1j * filtered_imag.astype(jnp.float32)).reshape(latitudes, modes, width)
        back = jnp.fft.ifft(filtered, axis=0) * latitudes
        back_real = rounded(back.real)
        back_imag = rounded(back.imag)
        padded = jnp.pad(back_real.astype(jnp.float32) + 1j * back_imag.astype(jnp.float32), ((0, 0), (0, 1), (0, 0)))
        spatial = rounded(jnp.fft.irfft(padded, n=longitudes, axis=1) * (longitudes * scale))
        mixed = (spatial.astype(jnp.float32) + normed.astype(jnp.float32)).astype(jnp.bfloat16)
        cot_values = cot_field.astype(jnp.float32)
        cot_lon = jnp.fft.rfft(cot_values, axis=1)[:, :modes]
        cot_real = rounded(cot_lon.real * scale)
        cot_imag = rounded(cot_lon.imag * scale)
        cot_spec = jnp.fft.fft(cot_real.astype(jnp.float32) + 1j * cot_imag.astype(jnp.float32), axis=0)
        grad_filt_real = rounded(cot_spec.real * mode_weights[None, :, None]).reshape(-1, blocks, block_size)
        grad_filt_imag = rounded(cot_spec.imag * mode_weights[None, :, None]).reshape(-1, blocks, block_size)
        grad_hid_real = block_adjoint(grad_filt_real, weight_two[0]) + block_adjoint(grad_filt_imag, weight_two[1])
        grad_hid_imag = block_adjoint(grad_filt_imag, weight_two[0]) - block_adjoint(grad_filt_real, weight_two[1])
        grad_before_real = rounded(grad_hid_real * gelu_slope(before_real))
        grad_before_imag = rounded(grad_hid_imag * gelu_slope(before_imag))
        grad_spec_real = rounded(block_adjoint(grad_before_real, weight_one[0]) + block_adjoint(grad_before_imag, weight_one[1]))
        grad_spec_imag = rounded(block_adjoint(grad_before_imag, weight_one[0]) - block_adjoint(grad_before_real, weight_one[1]))
        second = jnp.stack([block_outer(hidden_real, grad_filt_real) + block_outer(hidden_imag, grad_filt_imag), block_outer(hidden_real, grad_filt_imag) - block_outer(hidden_imag, grad_filt_real)])
        first = jnp.stack([block_outer(spec_real, grad_before_real) + block_outer(spec_imag, grad_before_imag), block_outer(spec_real, grad_before_imag) - block_outer(spec_imag, grad_before_real)])
        grad_spec = (grad_spec_real.astype(jnp.float32) + 1j * grad_spec_imag.astype(jnp.float32)).reshape(latitudes, modes, width)
        grad_back = jnp.fft.ifft(grad_spec, axis=0) * latitudes
        grad_back_real = rounded(grad_back.real)
        grad_back_imag = rounded(grad_back.imag)
        unweighted = (grad_back_real.astype(jnp.float32) + 1j * grad_back_imag.astype(jnp.float32)) / mode_weights[None, :, None]
        grad_padded = jnp.pad(unweighted, ((0, 0), (0, 1), (0, 0)))
        grad_field = rounded(jnp.fft.irfft(grad_padded, n=longitudes, axis=1) * (longitudes * scale))
        grad_normed = cot_values + grad_field.astype(jnp.float32)
        gain_part = lax.optimization_barrier(jnp.sum(grad_normed * standard, axis=(0, 1)))
        grad_hat = grad_normed * gain
        grad_in = inv_dev * (grad_hat - lax.optimization_barrier(jnp.mean(grad_hat, axis=-1, keepdims=True)) - standard * lax.optimization_barrier(jnp.mean(grad_hat * standard, axis=-1, keepdims=True)))
        return (mixed, grad_in.astype(jnp.bfloat16), first, second, gain_part)
    flat_tokens = tokens.reshape(members * samples, latitudes, longitudes, width)
    flat_cot = cotangent.reshape(members * samples, latitudes, longitudes, width)
    mixed, grad_in, first, second, gain_part = lax.map(one_sample, (flat_tokens, flat_cot))
    row_factor = 1.0 / math.sqrt(members * samples * latitudes * modes)
    token_factor = 1.0 / math.sqrt(members * samples * latitudes * longitudes)
    shape = (members, samples, latitudes, longitudes, width)
    return (mixed.reshape(shape), grad_in.reshape(shape), lax.optimization_barrier(jnp.sum(first, axis=0)) * row_factor, lax.optimization_barrier(jnp.sum(second, axis=0)) * row_factor, lax.optimization_barrier(jnp.sum(gain_part, axis=0)) * token_factor)
```

```python
import math

import jax
import jax.numpy as jnp
from jax import lax
from jax.sharding import Mesh
from jax.sharding import PartitionSpec as P

eps_norm = 1e-05
gelu_coef = 0.044715
GROUP = 8


def rounded(value):
    return lax.optimization_barrier(value.astype(jnp.bfloat16))


def gelu_value(value):
    factor = math.sqrt(2.0 / math.pi)
    return 0.5 * value * (1.0 + jnp.tanh(factor * (value + gelu_coef * value * value * value)))


def gelu_slope(value):
    factor = math.sqrt(2.0 / math.pi)
    tangent = jnp.tanh(factor * (value + gelu_coef * value * value * value))
    return 0.5 * (1.0 + tangent) + 0.5 * value * (1.0 - tangent * tangent) * factor * (
        1.0 + 3.0 * gelu_coef * value * value
    )


def table_parts(table):
    leading = table.astype(jnp.bfloat16)
    remainder = (table - leading.astype(jnp.float32)).astype(jnp.bfloat16)
    return (leading, remainder)


def data_table(form, data, parts):
    return jnp.einsum(form, data, parts[0], preferred_element_type=jnp.float32) + jnp.einsum(
        form, data, parts[1], preferred_element_type=jnp.float32
    )


def table_data(form, parts, data):
    return jnp.einsum(form, parts[0], data, preferred_element_type=jnp.float32) + jnp.einsum(
        form, parts[1], data, preferred_element_type=jnp.float32
    )


def longitude_tables(length, weights):
    places = jnp.arange(length, dtype=jnp.int32)
    numbers = jnp.arange(length // 2, dtype=jnp.int32)
    product = places[:, None] * numbers[None, :] % length
    angle = product.astype(jnp.float32) * (2.0 * math.pi / length)
    return (
        table_parts(jnp.cos(angle) * weights[None, :]),
        table_parts(jnp.sin(angle) * weights[None, :]),
    )


def latitude_tables(length):
    places = jnp.arange(length, dtype=jnp.int32)
    product = places[:, None] * places[None, :] % length
    angle = product.astype(jnp.float32) * (2.0 * math.pi / length)
    return (table_parts(jnp.cos(angle)), table_parts(jnp.sin(angle)))


def longitude_forward(field, cosine, sine, scale):
    real = data_table("nshwc,wk->nshkc", field, cosine) * scale
    imag = -data_table("nshwc,wk->nshkc", field, sine) * scale
    return (real, imag)


def longitude_inverse(real, imag, cosine, sine, scale):
    first = data_table("shkc,wk->shwc", real, cosine)
    second = data_table("shkc,wk->shwc", imag, sine)
    return (first - second) * scale


def latitude_forward(real, imag, cosine, sine):
    out_real = table_data("ah,nshkc->nsakc", cosine, real) + table_data("ah,nshkc->nsakc", sine, imag)
    out_imag = table_data("ah,nshkc->nsakc", cosine, imag) - table_data("ah,nshkc->nsakc", sine, real)
    return (out_real, out_imag)


def latitude_inverse(real, imag, cosine, sine):
    out_real = table_data("ah,nsakc->nshkc", cosine, real) - table_data("ah,nsakc->nshkc", sine, imag)
    out_imag = table_data("ah,nsakc->nshkc", cosine, imag) + table_data("ah,nsakc->nshkc", sine, real)
    return (out_real, out_imag)


def product(rows, weight):
    return jnp.dot(rows, weight, preferred_element_type=jnp.float32)


def adjoint(rows, weight):
    return lax.dot_general(rows, weight, (((1,), (1,)), ((), ())), preferred_element_type=jnp.float32)


def outer(left, right):
    return lax.dot_general(left, right, (((0,), (0,)), ((), ())), preferred_element_type=jnp.float32)


LON = ("lhi", "llo")


def body(tokens, cotangent, gain, weight_one, weight_two, bias_one, bias_two):
    field = tokens[0]
    cot_field = cotangent[0]
    samples, latitudes, local_width, width = field.shape
    lon_count = lax.axis_size(LON)
    group = lax.axis_size("llo")
    member_count = lax.axis_size("ens")
    full_width = local_width * lon_count
    modes = full_width // 2
    blocks = weight_one.shape[1]
    block_size = weight_one.shape[2]
    group_modes = modes // group
    block = lax.axis_index("lhi")
    member = lax.axis_index("ens")
    scale = 1.0 / math.sqrt(latitudes * full_width)
    full_weights = jnp.where(jnp.arange(modes) == 0, 1.0, 2.0).astype(jnp.float32)
    unit_weights = jnp.ones((modes,), jnp.float32)
    lon_cosine, lon_sine = longitude_tables(full_width, unit_weights)
    wide_cosine, wide_sine = longitude_tables(full_width, full_weights)
    lat_cosine, lat_sine = latitude_tables(latitudes)

    w1 = lax.dynamic_index_in_dim(weight_one, block, 1, keepdims=False)
    w2 = lax.dynamic_index_in_dim(weight_two, block, 1, keepdims=False)
    b1 = lax.dynamic_slice_in_dim(bias_one, block * block_size, block_size, 1)
    b2 = lax.dynamic_slice_in_dim(bias_two, block * block_size, block_size, 1)

    values = field.astype(jnp.float32)
    center = values - jnp.mean(values, axis=-1, keepdims=True)
    inv_dev = lax.rsqrt(jnp.mean(center * center, axis=-1, keepdims=True) + eps_norm)
    standard = center * inv_dev
    normed = (standard * gain).astype(jnp.bfloat16)

    both = jnp.stack([normed, cot_field])
    cols = lax.all_to_all(both, LON, split_axis=4, concat_axis=3, tiled=True)
    part_real, part_imag = longitude_forward(cols, lon_cosine, lon_sine, scale)
    part_real = rounded(part_real)
    part_imag = rounded(part_imag)
    spec_real, spec_imag = latitude_forward(part_real, part_imag, lat_cosine, lat_sine)
    kw_weights = full_weights[None, None, :, None]
    stacked = jnp.stack(
        [
            spec_real[0].astype(jnp.bfloat16),
            spec_imag[0].astype(jnp.bfloat16),
            (spec_real[1] * kw_weights).astype(jnp.bfloat16),
            (spec_imag[1] * kw_weights).astype(jnp.bfloat16),
        ]
    )
    local = lax.all_to_all(stacked, "llo", split_axis=3, concat_axis=4, tiled=True)
    local_shape = local.shape[1:]
    rows = local.reshape(4, -1, block_size)
    rows_real, rows_imag, rows_filt_real, rows_filt_imag = rows[0], rows[1], rows[2], rows[3]

    before_real = product(rows_real, w1[0]) - product(rows_imag, w1[1]) + b1[0]
    before_imag = product(rows_imag, w1[0]) + product(rows_real, w1[1]) + b1[1]
    hidden_real = gelu_value(before_real).astype(jnp.bfloat16)
    hidden_imag = gelu_value(before_imag).astype(jnp.bfloat16)
    filtered_real = (product(hidden_real, w2[0]) - product(hidden_imag, w2[1]) + b2[0]).astype(
        jnp.bfloat16
    )
    filtered_imag = (product(hidden_imag, w2[0]) + product(hidden_real, w2[1]) + b2[1]).astype(
        jnp.bfloat16
    )

    grad_hid_real = adjoint(rows_filt_real, w2[0]) + adjoint(rows_filt_imag, w2[1])
    grad_hid_imag = adjoint(rows_filt_imag, w2[0]) - adjoint(rows_filt_real, w2[1])
    grad_before_real = (grad_hid_real * gelu_slope(before_real)).astype(jnp.bfloat16)
    grad_before_imag = (grad_hid_imag * gelu_slope(before_imag)).astype(jnp.bfloat16)
    grad_spec_real = (
        adjoint(grad_before_real, w1[0]) + adjoint(grad_before_imag, w1[1])
    ).astype(jnp.bfloat16)
    grad_spec_imag = (
        adjoint(grad_before_imag, w1[0]) - adjoint(grad_before_real, w1[1])
    ).astype(jnp.bfloat16)
    second = jnp.stack(
        [
            outer(hidden_real, rows_filt_real) + outer(hidden_imag, rows_filt_imag),
            outer(hidden_real, rows_filt_imag) - outer(hidden_imag, rows_filt_real),
        ]
    )
    first = jnp.stack(
        [
            outer(rows_real, grad_before_real) + outer(rows_imag, grad_before_imag),
            outer(rows_real, grad_before_imag) - outer(rows_imag, grad_before_real),
        ]
    )

    back_stack = jnp.stack([filtered_real, filtered_imag, grad_spec_real, grad_spec_imag])
    back_stack = back_stack.reshape((4,) + local_shape)
    moved = lax.all_to_all(back_stack, "llo", split_axis=4, concat_axis=3, tiled=True)
    back_real, back_imag = latitude_inverse(
        moved[0::2], moved[1::2], lat_cosine, lat_sine
    )
    back_real = rounded(back_real)
    back_imag = rounded(back_imag)
    spatial = longitude_inverse(back_real[0], back_imag[0], wide_cosine, wide_sine, scale)
    grad_spatial = longitude_inverse(back_real[1], back_imag[1], lon_cosine, lon_sine, scale)
    out_stack = jnp.stack([spatial.astype(jnp.bfloat16), grad_spatial.astype(jnp.bfloat16)])
    out_tokens = lax.all_to_all(out_stack, LON, split_axis=3, concat_axis=4, tiled=True)
    spatial_tokens = out_tokens[0]
    grad_field = out_tokens[1]

    mixed = (spatial_tokens.astype(jnp.float32) + normed.astype(jnp.float32)).astype(jnp.bfloat16)
    grad_normed = cot_field.astype(jnp.float32) + grad_field.astype(jnp.float32)
    gain_row = jnp.sum(grad_normed * standard, axis=(0, 1, 2))
    grad_hat = grad_normed * gain
    grad_in = inv_dev * (
        grad_hat
        - jnp.mean(grad_hat, axis=-1, keepdims=True)
        - standard * jnp.mean(grad_hat * standard, axis=-1, keepdims=True)
    )

    weight_count = 2 * block_size * block_size
    payload = jnp.concatenate([first.reshape(-1), second.reshape(-1), gain_row])
    payload = lax.psum(payload, ("ens", "llo"))
    gathered = lax.all_gather(payload, "lhi")
    share = blocks // member_count
    gain_share = width // member_count
    row_factor = 1.0 / math.sqrt(member_count * samples * latitudes * modes)
    token_factor = 1.0 / math.sqrt(member_count * samples * latitudes * full_width)
    weights_part = gathered[:, : 2 * weight_count].reshape(blocks, 2, 2, block_size, block_size)
    mine = lax.dynamic_slice_in_dim(weights_part, member * share, share, 0)
    sum_first = jnp.transpose(mine[:, 0], (1, 0, 2, 3))
    sum_second = jnp.transpose(mine[:, 1], (1, 0, 2, 3))
    sum_gain = jnp.sum(gathered[:, 2 * weight_count :], axis=0)
    sum_gain = lax.dynamic_slice_in_dim(sum_gain, member * gain_share, gain_share, 0)
    return (
        mixed[None],
        grad_in.astype(jnp.bfloat16)[None],
        sum_first * row_factor,
        sum_second * row_factor,
        sum_gain * token_factor,
    )


def solution(mesh):
    ens_size, lon_size = mesh.devices.shape
    view = Mesh(
        mesh.devices.reshape(ens_size, lon_size // GROUP, GROUP), ("ens", "lhi", "llo")
    )
    token_spec = P("ens", None, None, LON, None)
    return jax.shard_map(
        body,
        mesh=view,
        in_specs=(token_spec, token_spec, P(), P(), P(), P(), P()),
        out_specs=(
            token_spec,
            token_spec,
            P(None, "ens", None, None),
            P(None, "ens", None, None),
            P("ens"),
        ),
        check_vma=False,
    )
```

```python
import math

import jax
import jax.numpy as jnp
from jax import lax
from jax.sharding import Mesh
from jax.sharding import PartitionSpec as P

eps_norm = 1e-05
gelu_coef = 0.044715
GROUP = 8


def rounded(value):
    return lax.optimization_barrier(value.astype(jnp.bfloat16))


def gelu_value(value):
    factor = math.sqrt(2.0 / math.pi)
    return 0.5 * value * (1.0 + jnp.tanh(factor * (value + gelu_coef * value * value * value)))


def gelu_slope(value):
    factor = math.sqrt(2.0 / math.pi)
    tangent = jnp.tanh(factor * (value + gelu_coef * value * value * value))
    return 0.5 * (1.0 + tangent) + 0.5 * value * (1.0 - tangent * tangent) * factor * (
        1.0 + 3.0 * gelu_coef * value * value
    )


def table_parts(table):
    leading = table.astype(jnp.bfloat16)
    remainder = (table - leading.astype(jnp.float32)).astype(jnp.bfloat16)
    return (leading, remainder)


def data_table(form, data, parts):
    return jnp.einsum(form, data, parts[0], preferred_element_type=jnp.float32) + jnp.einsum(
        form, data, parts[1], preferred_element_type=jnp.float32
    )


def table_data(form, parts, data):
    return jnp.einsum(form, parts[0], data, preferred_element_type=jnp.float32) + jnp.einsum(
        form, parts[1], data, preferred_element_type=jnp.float32
    )


def longitude_tables(length, weights):
    places = jnp.arange(length, dtype=jnp.int32)
    numbers = jnp.arange(length // 2, dtype=jnp.int32)
    product = places[:, None] * numbers[None, :] % length
    angle = product.astype(jnp.float32) * (2.0 * math.pi / length)
    return (
        table_parts(jnp.cos(angle) * weights[None, :]),
        table_parts(jnp.sin(angle) * weights[None, :]),
    )


def latitude_tables(length):
    places = jnp.arange(length, dtype=jnp.int32)
    product = places[:, None] * places[None, :] % length
    angle = product.astype(jnp.float32) * (2.0 * math.pi / length)
    return (table_parts(jnp.cos(angle)), table_parts(jnp.sin(angle)))


def longitude_forward(field, cosine, sine, scale):
    real = data_table("nshwc,wk->nshkc", field, cosine) * scale
    imag = -data_table("nshwc,wk->nshkc", field, sine) * scale
    return (real, imag)


def longitude_inverse(real, imag, cosine, sine, scale):
    first = data_table("shkc,wk->shwc", real, cosine)
    second = data_table("shkc,wk->shwc", imag, sine)
    return (first - second) * scale


def latitude_forward(real, imag, cosine, sine):
    out_real = table_data("ah,nshkc->nsakc", cosine, real) + table_data("ah,nshkc->nsakc", sine, imag)
    out_imag = table_data("ah,nshkc->nsakc", cosine, imag) - table_data("ah,nshkc->nsakc", sine, real)
    return (out_real, out_imag)


def latitude_inverse(real, imag, cosine, sine):
    out_real = table_data("ah,nsakc->nshkc", cosine, real) - table_data("ah,nsakc->nshkc", sine, imag)
    out_imag = table_data("ah,nsakc->nshkc", cosine, imag) + table_data("ah,nsakc->nshkc", sine, real)
    return (out_real, out_imag)


def product(rows, weight):
    return jnp.dot(rows, weight, preferred_element_type=jnp.float32)


def adjoint(rows, weight):
    return lax.dot_general(rows, weight, (((1,), (1,)), ((), ())), preferred_element_type=jnp.float32)


def outer(left, right):
    return lax.dot_general(left, right, (((0,), (0,)), ((), ())), preferred_element_type=jnp.float32)


LON = ("lhi", "llo")


def body(tokens, cotangent, gain, weight_one, weight_two, bias_one, bias_two):
    field = tokens[0]
    cot_field = cotangent[0]
    samples, latitudes, local_width, width = field.shape
    lon_count = lax.axis_size(LON)
    group = lax.axis_size("llo")
    member_count = lax.axis_size("ens")
    full_width = local_width * lon_count
    modes = full_width // 2
    blocks = weight_one.shape[1]
    block_size = weight_one.shape[2]
    group_modes = modes // group
    block = lax.axis_index("lhi")
    member = lax.axis_index("ens")
    scale = 1.0 / math.sqrt(latitudes * full_width)
    full_weights = jnp.where(jnp.arange(modes) == 0, 1.0, 2.0).astype(jnp.float32)
    unit_weights = jnp.ones((modes,), jnp.float32)
    lon_cosine, lon_sine = longitude_tables(full_width, unit_weights)
    wide_cosine, wide_sine = longitude_tables(full_width, full_weights)
    lat_cosine, lat_sine = latitude_tables(latitudes)

    w1 = lax.dynamic_index_in_dim(weight_one, block, 1, keepdims=False)
    w2 = lax.dynamic_index_in_dim(weight_two, block, 1, keepdims=False)
    b1 = lax.dynamic_slice_in_dim(bias_one, block * block_size, block_size, 1)
    b2 = lax.dynamic_slice_in_dim(bias_two, block * block_size, block_size, 1)

    values = field.astype(jnp.float32)
    center = values - jnp.mean(values, axis=-1, keepdims=True)
    inv_dev = lax.rsqrt(jnp.mean(center * center, axis=-1, keepdims=True) + eps_norm)
    standard = center * inv_dev
    normed = (standard * gain).astype(jnp.bfloat16)

    both = jnp.stack([normed, cot_field])
    cols = lax.all_to_all(both, LON, split_axis=4, concat_axis=3, tiled=True)
    part_real, part_imag = longitude_forward(cols, lon_cosine, lon_sine, scale)
    part_real = rounded(part_real)
    part_imag = rounded(part_imag)
    spec_real, spec_imag = latitude_forward(part_real, part_imag, lat_cosine, lat_sine)
    kw_weights = full_weights[None, None, :, None]
    stacked = jnp.stack(
        [
            spec_real[0].astype(jnp.bfloat16),
            spec_imag[0].astype(jnp.bfloat16),
            (spec_real[1] * kw_weights).astype(jnp.bfloat16),
            (spec_imag[1] * kw_weights).astype(jnp.bfloat16),
        ]
    )
    local = lax.all_to_all(stacked, "llo", split_axis=3, concat_axis=4, tiled=True)
    local_shape = local.shape[1:]
    rows = local.reshape(4, -1, block_size)
    rows_real, rows_imag, rows_filt_real, rows_filt_imag = rows[0], rows[1], rows[2], rows[3]

    before_real = product(rows_real, w1[0]) - product(rows_imag, w1[1]) + b1[0]
    before_imag = product(rows_imag, w1[0]) + product(rows_real, w1[1]) + b1[1]
    hidden_real = gelu_value(before_real).astype(jnp.bfloat16)
    hidden_imag = gelu_value(before_imag).astype(jnp.bfloat16)
    filtered_real = (product(hidden_real, w2[0]) - product(hidden_imag, w2[1]) + b2[0]).astype(
        jnp.bfloat16
    )
    filtered_imag = (product(hidden_imag, w2[0]) + product(hidden_real, w2[1]) + b2[1]).astype(
        jnp.bfloat16
    )

    grad_hid_real = adjoint(rows_filt_real, w2[0]) + adjoint(rows_filt_imag, w2[1])
    grad_hid_imag = adjoint(rows_filt_imag, w2[0]) - adjoint(rows_filt_real, w2[1])
    grad_before_real = (grad_hid_real * gelu_slope(before_real)).astype(jnp.bfloat16)
    grad_before_imag = (grad_hid_imag * gelu_slope(before_imag)).astype(jnp.bfloat16)
    grad_spec_real = (
        adjoint(grad_before_real, w1[0]) + adjoint(grad_before_imag, w1[1])
    ).astype(jnp.bfloat16)
    grad_spec_imag = (
        adjoint(grad_before_imag, w1[0]) - adjoint(grad_before_real, w1[1])
    ).astype(jnp.bfloat16)
    second = jnp.stack(
        [
            outer(hidden_real, rows_filt_real) + outer(hidden_imag, rows_filt_imag),
            outer(hidden_real, rows_filt_imag) - outer(hidden_imag, rows_filt_real),
        ]
    )
    first = jnp.stack(
        [
            outer(rows_real, grad_before_real) + outer(rows_imag, grad_before_imag),
            outer(rows_real, grad_before_imag) - outer(rows_imag, grad_before_real),
        ]
    )

    back_stack = jnp.stack([filtered_real, filtered_imag, grad_spec_real, grad_spec_imag])
    back_stack = back_stack.reshape((4,) + local_shape)
    moved = lax.all_to_all(back_stack, "llo", split_axis=4, concat_axis=3, tiled=True)
    back_real, back_imag = latitude_inverse(
        moved[0::2], moved[1::2], lat_cosine, lat_sine
    )
    back_real = rounded(back_real)
    back_imag = rounded(back_imag)
    spatial = longitude_inverse(back_real[0], back_imag[0], wide_cosine, wide_sine, scale)
    grad_spatial = longitude_inverse(back_real[1], back_imag[1], lon_cosine, lon_sine, scale)
    out_stack = jnp.stack([spatial.astype(jnp.bfloat16), grad_spatial.astype(jnp.bfloat16)])
    out_tokens = lax.all_to_all(out_stack, LON, split_axis=3, concat_axis=4, tiled=True)
    spatial_tokens = out_tokens[0]
    grad_field = out_tokens[1]

    mixed = (spatial_tokens.astype(jnp.float32) + normed.astype(jnp.float32)).astype(jnp.bfloat16)
    grad_normed = cot_field.astype(jnp.float32) + grad_field.astype(jnp.float32)
    gain_row = jnp.sum(grad_normed * standard, axis=(0, 1, 2))
    grad_hat = grad_normed * gain
    grad_in = inv_dev * (
        grad_hat
        - jnp.mean(grad_hat, axis=-1, keepdims=True)
        - standard * jnp.mean(grad_hat * standard, axis=-1, keepdims=True)
    )

    share = blocks // member_count
    gain_share = width // member_count
    row_factor = 1.0 / math.sqrt(member_count * samples * latitudes * modes)
    token_factor = 1.0 / math.sqrt(member_count * samples * latitudes * full_width)
    pieces = group * member_count
    weight_size = 2 * 2 * block_size * block_size
    weight_piece = weight_size // pieces
    gain_piece = width // pieces
    payload = jnp.concatenate(
        [
            jnp.concatenate([first.reshape(-1), second.reshape(-1)]).reshape(group, member_count, weight_piece),
            gain_row.reshape(group, member_count, gain_piece),
        ],
        axis=2,
    )
    summed = jnp.sum(lax.all_to_all(payload, "llo", split_axis=0, concat_axis=0, tiled=True), axis=0)
    summed = jnp.sum(lax.all_to_all(summed, "ens", split_axis=0, concat_axis=0, tiled=True), axis=0)
    dest_member = jnp.arange(member_count * blocks)[:, None] // blocks
    keep = (dest_member == block // share).astype(jnp.float32)
    routed = jnp.concatenate(
        [
            keep * summed[None, :weight_piece],
            jnp.broadcast_to(summed[None, weight_piece:], (member_count * blocks, gain_piece)),
        ],
        axis=1,
    )
    routed = lax.all_to_all(routed, ("ens", "lhi"), split_axis=0, concat_axis=0, tiled=True)
    routed = routed.reshape(member_count, blocks, weight_piece + gain_piece)
    mine = lax.dynamic_slice_in_dim(routed[:, :, :weight_piece], member * share, share, 1)
    gain_part = jnp.sum(routed[:, :, weight_piece:], axis=1)
    local_result = jnp.concatenate([mine.reshape(member_count, share * weight_piece), gain_part], axis=1)
    spread = jnp.broadcast_to(local_result[None], (group,) + local_result.shape)
    spread = lax.all_to_all(spread, "llo", split_axis=0, concat_axis=0, tiled=True)
    weights_all = spread[:, :, : share * weight_piece].reshape(group, member_count, share, weight_piece)
    weights_all = jnp.transpose(weights_all, (2, 0, 1, 3)).reshape(share, 2, 2, block_size, block_size)
    sum_first = jnp.transpose(weights_all[:, 0], (1, 0, 2, 3))
    sum_second = jnp.transpose(weights_all[:, 1], (1, 0, 2, 3))
    sum_gain = spread[:, :, share * weight_piece :].reshape(width)
    sum_gain = lax.dynamic_slice_in_dim(sum_gain, member * gain_share, gain_share, 0)
    return (
        mixed[None],
        grad_in.astype(jnp.bfloat16)[None],
        sum_first * row_factor,
        sum_second * row_factor,
        sum_gain * token_factor,
    )


def solution(mesh):
    ens_size, lon_size = mesh.devices.shape
    view = Mesh(
        mesh.devices.reshape(ens_size, lon_size // GROUP, GROUP), ("ens", "lhi", "llo")
    )
    token_spec = P("ens", None, None, LON, None)
    return jax.shard_map(
        body,
        mesh=view,
        in_specs=(token_spec, token_spec, P(), P(), P(), P(), P()),
        out_specs=(
            token_spec,
            token_spec,
            P(None, "ens", None, None),
            P(None, "ens", None, None),
            P("ens"),
        ),
        check_vma=False,
    )
```

```python
import math

import jax
import jax.numpy as jnp
from jax import lax
from jax.sharding import Mesh
from jax.sharding import PartitionSpec as P

eps_norm = 1e-05
gelu_coef = 0.044715
GROUP = 8


def rounded(value):
    return lax.optimization_barrier(value.astype(jnp.bfloat16))


def gelu_value(value):
    factor = math.sqrt(2.0 / math.pi)
    return 0.5 * value * (1.0 + jnp.tanh(factor * (value + gelu_coef * value * value * value)))


def gelu_slope(value):
    factor = math.sqrt(2.0 / math.pi)
    tangent = jnp.tanh(factor * (value + gelu_coef * value * value * value))
    return 0.5 * (1.0 + tangent) + 0.5 * value * (1.0 - tangent * tangent) * factor * (
        1.0 + 3.0 * gelu_coef * value * value
    )


def table_parts(table):
    leading = table.astype(jnp.bfloat16)
    remainder = (table - leading.astype(jnp.float32)).astype(jnp.bfloat16)
    return (leading, remainder)


def data_table(form, data, parts):
    return jnp.einsum(form, data, parts[0], preferred_element_type=jnp.float32) + jnp.einsum(
        form, data, parts[1], preferred_element_type=jnp.float32
    )


def table_data(form, parts, data):
    return jnp.einsum(form, parts[0], data, preferred_element_type=jnp.float32) + jnp.einsum(
        form, parts[1], data, preferred_element_type=jnp.float32
    )


def longitude_tables(length, weights):
    places = jnp.arange(length, dtype=jnp.int32)
    numbers = jnp.arange(length // 2, dtype=jnp.int32)
    product = places[:, None] * numbers[None, :] % length
    angle = product.astype(jnp.float32) * (2.0 * math.pi / length)
    return (
        table_parts(jnp.cos(angle) * weights[None, :]),
        table_parts(jnp.sin(angle) * weights[None, :]),
    )


def latitude_tables(length):
    places = jnp.arange(length, dtype=jnp.int32)
    product = places[:, None] * places[None, :] % length
    angle = product.astype(jnp.float32) * (2.0 * math.pi / length)
    return (table_parts(jnp.cos(angle)), table_parts(jnp.sin(angle)))


def longitude_forward(field, cosine, sine, scale):
    real = data_table("nshwc,wk->nshkc", field, cosine) * scale
    imag = -data_table("nshwc,wk->nshkc", field, sine) * scale
    return (real, imag)


def longitude_inverse(real, imag, cosine, sine, scale):
    first = data_table("shkc,wk->shwc", real, cosine)
    second = data_table("shkc,wk->shwc", imag, sine)
    return (first - second) * scale


def latitude_forward(real, imag, cosine, sine):
    out_real = table_data("ah,nshkc->nsakc", cosine, real) + table_data("ah,nshkc->nsakc", sine, imag)
    out_imag = table_data("ah,nshkc->nsakc", cosine, imag) - table_data("ah,nshkc->nsakc", sine, real)
    return (out_real, out_imag)


def latitude_inverse(real, imag, cosine, sine):
    out_real = table_data("ah,nsakc->nshkc", cosine, real) - table_data("ah,nsakc->nshkc", sine, imag)
    out_imag = table_data("ah,nsakc->nshkc", cosine, imag) + table_data("ah,nsakc->nshkc", sine, real)
    return (out_real, out_imag)


def product(rows, weight):
    return jnp.dot(rows, weight, preferred_element_type=jnp.float32)


def adjoint(rows, weight):
    return lax.dot_general(rows, weight, (((1,), (1,)), ((), ())), preferred_element_type=jnp.float32)


def outer(left, right):
    return lax.dot_general(left, right, (((0,), (0,)), ((), ())), preferred_element_type=jnp.float32)


LON = ("lhi", "llo")


def body(tokens, cotangent, gain, weight_one, weight_two, bias_one, bias_two):
    field = tokens[0]
    cot_field = cotangent[0]
    samples, latitudes, local_width, width = field.shape
    lon_count = lax.axis_size(LON)
    group = lax.axis_size("llo")
    member_count = lax.axis_size("ens")
    full_width = local_width * lon_count
    modes = full_width // 2
    blocks = weight_one.shape[1]
    block_size = weight_one.shape[2]
    group_modes = modes // group
    block = lax.axis_index("lhi")
    member = lax.axis_index("ens")
    scale = 1.0 / math.sqrt(latitudes * full_width)
    full_weights = jnp.where(jnp.arange(modes) == 0, 1.0, 2.0).astype(jnp.float32)
    unit_weights = jnp.ones((modes,), jnp.float32)
    lon_cosine, lon_sine = longitude_tables(full_width, unit_weights)
    wide_cosine, wide_sine = longitude_tables(full_width, full_weights)
    lat_cosine, lat_sine = latitude_tables(latitudes)

    w1 = lax.dynamic_index_in_dim(weight_one, block, 1, keepdims=False)
    w2 = lax.dynamic_index_in_dim(weight_two, block, 1, keepdims=False)
    b1 = lax.dynamic_slice_in_dim(bias_one, block * block_size, block_size, 1)
    b2 = lax.dynamic_slice_in_dim(bias_two, block * block_size, block_size, 1)

    values = field.astype(jnp.float32)
    center = values - jnp.mean(values, axis=-1, keepdims=True)
    inv_dev = lax.rsqrt(jnp.mean(center * center, axis=-1, keepdims=True) + eps_norm)
    standard = center * inv_dev
    normed = (standard * gain).astype(jnp.bfloat16)

    both = jnp.stack([normed, cot_field])
    cols = lax.all_to_all(both, LON, split_axis=4, concat_axis=3, tiled=True)
    part_real, part_imag = longitude_forward(cols, lon_cosine, lon_sine, scale)
    part_real = rounded(part_real)
    part_imag = rounded(part_imag)
    spec_real, spec_imag = latitude_forward(part_real, part_imag, lat_cosine, lat_sine)
    kw_weights = full_weights[None, None, :, None]
    stacked = jnp.stack(
        [
            spec_real[0].astype(jnp.bfloat16),
            spec_imag[0].astype(jnp.bfloat16),
            (spec_real[1] * kw_weights).astype(jnp.bfloat16),
            (spec_imag[1] * kw_weights).astype(jnp.bfloat16),
        ]
    )
    local = lax.all_to_all(stacked, "llo", split_axis=3, concat_axis=4, tiled=True)
    local_shape = local.shape[1:]
    rows = local.reshape(4, -1, block_size)
    rows_real, rows_imag, rows_filt_real, rows_filt_imag = rows[0], rows[1], rows[2], rows[3]

    before_real = product(rows_real, w1[0]) - product(rows_imag, w1[1]) + b1[0]
    before_imag = product(rows_imag, w1[0]) + product(rows_real, w1[1]) + b1[1]
    hidden_real = gelu_value(before_real).astype(jnp.bfloat16)
    hidden_imag = gelu_value(before_imag).astype(jnp.bfloat16)
    filtered_real = (product(hidden_real, w2[0]) - product(hidden_imag, w2[1]) + b2[0]).astype(
        jnp.bfloat16
    )
    filtered_imag = (product(hidden_imag, w2[0]) + product(hidden_real, w2[1]) + b2[1]).astype(
        jnp.bfloat16
    )

    grad_hid_real = adjoint(rows_filt_real, w2[0]) + adjoint(rows_filt_imag, w2[1])
    grad_hid_imag = adjoint(rows_filt_imag, w2[0]) - adjoint(rows_filt_real, w2[1])
    grad_before_real = (grad_hid_real * gelu_slope(before_real)).astype(jnp.bfloat16)
    grad_before_imag = (grad_hid_imag * gelu_slope(before_imag)).astype(jnp.bfloat16)
    grad_spec_real = (
        adjoint(grad_before_real, w1[0]) + adjoint(grad_before_imag, w1[1])
    ).astype(jnp.bfloat16)
    grad_spec_imag = (
        adjoint(grad_before_imag, w1[0]) - adjoint(grad_before_real, w1[1])
    ).astype(jnp.bfloat16)
    second = jnp.stack(
        [
            outer(hidden_real, rows_filt_real) + outer(hidden_imag, rows_filt_imag),
            outer(hidden_real, rows_filt_imag) - outer(hidden_imag, rows_filt_real),
        ]
    )
    first = jnp.stack(
        [
            outer(rows_real, grad_before_real) + outer(rows_imag, grad_before_imag),
            outer(rows_real, grad_before_imag) - outer(rows_imag, grad_before_real),
        ]
    )

    back_stack = jnp.stack([filtered_real, filtered_imag, grad_spec_real, grad_spec_imag])
    back_stack = back_stack.reshape((4,) + local_shape)
    moved = lax.all_to_all(back_stack, "llo", split_axis=4, concat_axis=3, tiled=True)
    back_real, back_imag = latitude_inverse(
        moved[0::2], moved[1::2], lat_cosine, lat_sine
    )
    back_real = rounded(back_real)
    back_imag = rounded(back_imag)
    spatial = longitude_inverse(back_real[0], back_imag[0], wide_cosine, wide_sine, scale)
    grad_spatial = longitude_inverse(back_real[1], back_imag[1], lon_cosine, lon_sine, scale)
    out_stack = jnp.stack([spatial.astype(jnp.bfloat16), grad_spatial.astype(jnp.bfloat16)])
    out_tokens = lax.all_to_all(out_stack, LON, split_axis=3, concat_axis=4, tiled=True)
    spatial_tokens = out_tokens[0]
    grad_field = out_tokens[1]

    mixed = (spatial_tokens.astype(jnp.float32) + normed.astype(jnp.float32)).astype(jnp.bfloat16)
    grad_normed = cot_field.astype(jnp.float32) + grad_field.astype(jnp.float32)
    gain_row = jnp.sum(grad_normed * standard, axis=(0, 1, 2))
    grad_hat = grad_normed * gain
    grad_in = inv_dev * (
        grad_hat
        - jnp.mean(grad_hat, axis=-1, keepdims=True)
        - standard * jnp.mean(grad_hat * standard, axis=-1, keepdims=True)
    )

    share = blocks // member_count
    gain_share = width // member_count
    row_factor = 1.0 / math.sqrt(member_count * samples * latitudes * modes)
    token_factor = 1.0 / math.sqrt(member_count * samples * latitudes * full_width)
    pieces = group * member_count
    weight_size = 2 * 2 * block_size * block_size
    weight_piece = weight_size // pieces
    payload = jnp.concatenate([first.reshape(-1), second.reshape(-1)]).reshape(
        group, member_count, weight_piece
    )
    summed = jnp.sum(lax.all_to_all(payload, "llo", split_axis=0, concat_axis=0, tiled=True), axis=0)
    summed = jnp.sum(lax.all_to_all(summed, "ens", split_axis=0, concat_axis=0, tiled=True), axis=0)
    dest_member = jnp.arange(member_count * blocks)[:, None] // blocks
    keep = (dest_member == block // share).astype(jnp.float32)
    routed = lax.all_to_all(keep * summed[None, :], ("ens", "lhi"), split_axis=0, concat_axis=0, tiled=True)
    routed = routed.reshape(member_count, blocks, weight_piece)
    mine = lax.dynamic_slice_in_dim(routed, member * share, share, 1)
    local_result = mine.reshape(member_count, share * weight_piece)
    spread = jnp.broadcast_to(local_result[None], (group,) + local_result.shape)
    spread = lax.all_to_all(spread, "llo", split_axis=0, concat_axis=0, tiled=True)
    weights_all = spread.reshape(group, member_count, share, weight_piece)
    weights_all = jnp.transpose(weights_all, (2, 0, 1, 3)).reshape(share, 2, 2, block_size, block_size)
    sum_first = jnp.transpose(weights_all[:, 0], (1, 0, 2, 3))
    sum_second = jnp.transpose(weights_all[:, 1], (1, 0, 2, 3))

    devices = member_count * lon_count
    gain_rows = jnp.broadcast_to(
        gain_row.reshape(member_count, 1, gain_share), (member_count, devices // member_count, gain_share)
    ).reshape(devices, gain_share)
    gain_rows = lax.all_to_all(gain_rows, ("ens", "lhi", "llo"), split_axis=0, concat_axis=0, tiled=True)
    sum_gain = jnp.sum(gain_rows, axis=0)
    return (
        mixed[None],
        grad_in.astype(jnp.bfloat16)[None],
        sum_first * row_factor,
        sum_second * row_factor,
        sum_gain * token_factor,
    )


def solution(mesh):
    ens_size, lon_size = mesh.devices.shape
    view = Mesh(
        mesh.devices.reshape(ens_size, lon_size // GROUP, GROUP), ("ens", "lhi", "llo")
    )
    token_spec = P("ens", None, None, LON, None)
    return jax.shard_map(
        body,
        mesh=view,
        in_specs=(token_spec, token_spec, P(), P(), P(), P(), P()),
        out_specs=(
            token_spec,
            token_spec,
            P(None, "ens", None, None),
            P(None, "ens", None, None),
            P("ens"),
        ),
        check_vma=False,
    )
```

```python
import math

import jax
import jax.numpy as jnp
from jax import lax
from jax.sharding import Mesh
from jax.sharding import PartitionSpec as P

eps_norm = 1e-05
gelu_coef = 0.044715
GROUP = 8


def rounded(value):
    return lax.optimization_barrier(value.astype(jnp.bfloat16))


def gelu_value(value):
    factor = math.sqrt(2.0 / math.pi)
    return 0.5 * value * (1.0 + jnp.tanh(factor * (value + gelu_coef * value * value * value)))


def gelu_slope(value):
    factor = math.sqrt(2.0 / math.pi)
    tangent = jnp.tanh(factor * (value + gelu_coef * value * value * value))
    return 0.5 * (1.0 + tangent) + 0.5 * value * (1.0 - tangent * tangent) * factor * (
        1.0 + 3.0 * gelu_coef * value * value
    )


def table_parts(table):
    leading = table.astype(jnp.bfloat16)
    remainder = (table - leading.astype(jnp.float32)).astype(jnp.bfloat16)
    return (leading, remainder)


def data_table(form, data, parts):
    return jnp.einsum(form, data, parts[0], preferred_element_type=jnp.float32) + jnp.einsum(
        form, data, parts[1], preferred_element_type=jnp.float32
    )


def table_data(form, parts, data):
    return jnp.einsum(form, parts[0], data, preferred_element_type=jnp.float32) + jnp.einsum(
        form, parts[1], data, preferred_element_type=jnp.float32
    )


def longitude_tables(length, weights):
    places = jnp.arange(length, dtype=jnp.int32)
    numbers = jnp.arange(length // 2, dtype=jnp.int32)
    product = places[:, None] * numbers[None, :] % length
    angle = product.astype(jnp.float32) * (2.0 * math.pi / length)
    return (
        table_parts(jnp.cos(angle) * weights[None, :]),
        table_parts(jnp.sin(angle) * weights[None, :]),
    )


def latitude_tables(length):
    places = jnp.arange(length, dtype=jnp.int32)
    product = places[:, None] * places[None, :] % length
    angle = product.astype(jnp.float32) * (2.0 * math.pi / length)
    return (table_parts(jnp.cos(angle)), table_parts(jnp.sin(angle)))


def longitude_forward(field, cosine, sine, scale):
    real = data_table("nshwc,wk->nshkc", field, cosine) * scale
    imag = -data_table("nshwc,wk->nshkc", field, sine) * scale
    return (real, imag)


def longitude_inverse(real, imag, cosine, sine, scale):
    first = data_table("shkc,wk->shwc", real, cosine)
    second = data_table("shkc,wk->shwc", imag, sine)
    return (first - second) * scale


def latitude_forward(real, imag, cosine, sine):
    out_real = table_data("ah,nshkc->nsakc", cosine, real) + table_data("ah,nshkc->nsakc", sine, imag)
    out_imag = table_data("ah,nshkc->nsakc", cosine, imag) - table_data("ah,nshkc->nsakc", sine, real)
    return (out_real, out_imag)


def latitude_inverse(real, imag, cosine, sine):
    out_real = table_data("ah,nsakc->nshkc", cosine, real) - table_data("ah,nsakc->nshkc", sine, imag)
    out_imag = table_data("ah,nsakc->nshkc", cosine, imag) + table_data("ah,nsakc->nshkc", sine, real)
    return (out_real, out_imag)


def product(rows, weight):
    return jnp.dot(rows, weight, preferred_element_type=jnp.float32)


def adjoint(rows, weight):
    return lax.dot_general(rows, weight, (((1,), (1,)), ((), ())), preferred_element_type=jnp.float32)


def outer(left, right):
    return lax.dot_general(left, right, (((0,), (0,)), ((), ())), preferred_element_type=jnp.float32)


LON = ("lhi", "llo")


def body(tokens, cotangent, gain, weight_one, weight_two, bias_one, bias_two):
    field = tokens[0]
    cot_field = cotangent[0]
    samples, latitudes, local_width, width = field.shape
    lon_count = lax.axis_size(LON)
    group = lax.axis_size("llo")
    member_count = lax.axis_size("ens")
    full_width = local_width * lon_count
    modes = full_width // 2
    blocks = weight_one.shape[1]
    block_size = weight_one.shape[2]
    group_modes = modes // group
    block = lax.axis_index("lhi")
    member = lax.axis_index("ens")
    scale = 1.0 / math.sqrt(latitudes * full_width)
    full_weights = jnp.where(jnp.arange(modes) == 0, 1.0, 2.0).astype(jnp.float32)
    unit_weights = jnp.ones((modes,), jnp.float32)
    lon_cosine, lon_sine = longitude_tables(full_width, unit_weights)
    wide_cosine, wide_sine = longitude_tables(full_width, full_weights)
    lat_cosine, lat_sine = latitude_tables(latitudes)

    w1 = lax.dynamic_index_in_dim(weight_one, block, 1, keepdims=False)
    w2 = lax.dynamic_index_in_dim(weight_two, block, 1, keepdims=False)
    b1 = lax.dynamic_slice_in_dim(bias_one, block * block_size, block_size, 1)
    b2 = lax.dynamic_slice_in_dim(bias_two, block * block_size, block_size, 1)

    values = field.astype(jnp.float32)
    center = values - jnp.mean(values, axis=-1, keepdims=True)
    inv_dev = lax.rsqrt(jnp.mean(center * center, axis=-1, keepdims=True) + eps_norm)
    standard = center * inv_dev
    normed = (standard * gain).astype(jnp.bfloat16)

    both = jnp.stack([normed, cot_field])
    cols = lax.all_to_all(both, LON, split_axis=4, concat_axis=3, tiled=True)
    part_real, part_imag = longitude_forward(cols, lon_cosine, lon_sine, scale)
    part_real = rounded(part_real)
    part_imag = rounded(part_imag)
    spec_real, spec_imag = latitude_forward(part_real, part_imag, lat_cosine, lat_sine)
    kw_weights = full_weights[None, None, :, None]
    spectra = [
        spec_real[0].astype(jnp.bfloat16),
        spec_imag[0].astype(jnp.bfloat16),
        (spec_real[1] * kw_weights).astype(jnp.bfloat16),
        (spec_imag[1] * kw_weights).astype(jnp.bfloat16),
    ]
    spectra = [lax.all_to_all(x, "llo", split_axis=2, concat_axis=3, tiled=True) for x in spectra]
    local_shape = spectra[0].shape
    rows_real, rows_imag, rows_filt_real, rows_filt_imag = [x.reshape(-1, block_size) for x in spectra]

    before_real = product(rows_real, w1[0]) - product(rows_imag, w1[1]) + b1[0]
    before_imag = product(rows_imag, w1[0]) + product(rows_real, w1[1]) + b1[1]
    hidden_real = gelu_value(before_real).astype(jnp.bfloat16)
    hidden_imag = gelu_value(before_imag).astype(jnp.bfloat16)
    filtered_real = (product(hidden_real, w2[0]) - product(hidden_imag, w2[1]) + b2[0]).astype(
        jnp.bfloat16
    )
    filtered_imag = (product(hidden_imag, w2[0]) + product(hidden_real, w2[1]) + b2[1]).astype(
        jnp.bfloat16
    )

    grad_hid_real = adjoint(rows_filt_real, w2[0]) + adjoint(rows_filt_imag, w2[1])
    grad_hid_imag = adjoint(rows_filt_imag, w2[0]) - adjoint(rows_filt_real, w2[1])
    grad_before_real = (grad_hid_real * gelu_slope(before_real)).astype(jnp.bfloat16)
    grad_before_imag = (grad_hid_imag * gelu_slope(before_imag)).astype(jnp.bfloat16)
    grad_spec_real = (
        adjoint(grad_before_real, w1[0]) + adjoint(grad_before_imag, w1[1])
    ).astype(jnp.bfloat16)
    grad_spec_imag = (
        adjoint(grad_before_imag, w1[0]) - adjoint(grad_before_real, w1[1])
    ).astype(jnp.bfloat16)
    second = jnp.stack(
        [
            outer(hidden_real, rows_filt_real) + outer(hidden_imag, rows_filt_imag),
            outer(hidden_real, rows_filt_imag) - outer(hidden_imag, rows_filt_real),
        ]
    )
    first = jnp.stack(
        [
            outer(rows_real, grad_before_real) + outer(rows_imag, grad_before_imag),
            outer(rows_real, grad_before_imag) - outer(rows_imag, grad_before_real),
        ]
    )

    back_stack = jnp.stack([filtered_real, filtered_imag, grad_spec_real, grad_spec_imag])
    back_stack = back_stack.reshape((4,) + local_shape)
    moved = lax.all_to_all(back_stack, "llo", split_axis=4, concat_axis=3, tiled=True)
    back_real, back_imag = latitude_inverse(
        moved[0::2], moved[1::2], lat_cosine, lat_sine
    )
    back_real = rounded(back_real)
    back_imag = rounded(back_imag)
    spatial = longitude_inverse(back_real[0], back_imag[0], wide_cosine, wide_sine, scale)
    grad_spatial = longitude_inverse(back_real[1], back_imag[1], lon_cosine, lon_sine, scale)
    out_stack = jnp.stack([spatial.astype(jnp.bfloat16), grad_spatial.astype(jnp.bfloat16)])
    out_tokens = lax.all_to_all(out_stack, LON, split_axis=3, concat_axis=4, tiled=True)
    spatial_tokens = out_tokens[0]
    grad_field = out_tokens[1]

    mixed = (spatial_tokens.astype(jnp.float32) + normed.astype(jnp.float32)).astype(jnp.bfloat16)
    grad_normed = cot_field.astype(jnp.float32) + grad_field.astype(jnp.float32)
    gain_row = jnp.sum(grad_normed * standard, axis=(0, 1, 2))
    grad_hat = grad_normed * gain
    grad_in = inv_dev * (
        grad_hat
        - jnp.mean(grad_hat, axis=-1, keepdims=True)
        - standard * jnp.mean(grad_hat * standard, axis=-1, keepdims=True)
    )

    share = blocks // member_count
    gain_share = width // member_count
    row_factor = 1.0 / math.sqrt(member_count * samples * latitudes * modes)
    token_factor = 1.0 / math.sqrt(member_count * samples * latitudes * full_width)
    pieces = group * member_count
    weight_size = 2 * 2 * block_size * block_size
    weight_piece = weight_size // pieces
    payload = jnp.concatenate([first.reshape(-1), second.reshape(-1)]).reshape(
        group, member_count, weight_piece
    )
    summed = jnp.sum(lax.all_to_all(payload, "llo", split_axis=0, concat_axis=0, tiled=True), axis=0)
    summed = jnp.sum(lax.all_to_all(summed, "ens", split_axis=0, concat_axis=0, tiled=True), axis=0)
    dest_member = jnp.arange(member_count * blocks)[:, None] // blocks
    keep = (dest_member == block // share).astype(jnp.float32)
    routed = lax.all_to_all(keep * summed[None, :], ("ens", "lhi"), split_axis=0, concat_axis=0, tiled=True)
    routed = routed.reshape(member_count, blocks, weight_piece)
    mine = lax.dynamic_slice_in_dim(routed, member * share, share, 1)
    local_result = mine.reshape(member_count, share * weight_piece)
    spread = jnp.broadcast_to(local_result[None], (group,) + local_result.shape)
    spread = lax.all_to_all(spread, "llo", split_axis=0, concat_axis=0, tiled=True)
    weights_all = spread.reshape(group, member_count, share, weight_piece)
    weights_all = jnp.transpose(weights_all, (2, 0, 1, 3)).reshape(share, 2, 2, block_size, block_size)
    sum_first = jnp.transpose(weights_all[:, 0], (1, 0, 2, 3))
    sum_second = jnp.transpose(weights_all[:, 1], (1, 0, 2, 3))

    devices = member_count * lon_count
    gain_rows = jnp.broadcast_to(
        gain_row.reshape(member_count, 1, gain_share), (member_count, devices // member_count, gain_share)
    ).reshape(devices, gain_share)
    gain_rows = lax.all_to_all(gain_rows, ("ens", "lhi", "llo"), split_axis=0, concat_axis=0, tiled=True)
    sum_gain = jnp.sum(gain_rows, axis=0)
    return (
        mixed[None],
        grad_in.astype(jnp.bfloat16)[None],
        sum_first * row_factor,
        sum_second * row_factor,
        sum_gain * token_factor,
    )


def solution(mesh):
    ens_size, lon_size = mesh.devices.shape
    view = Mesh(
        mesh.devices.reshape(ens_size, lon_size // GROUP, GROUP), ("ens", "lhi", "llo")
    )
    token_spec = P("ens", None, None, LON, None)
    return jax.shard_map(
        body,
        mesh=view,
        in_specs=(token_spec, token_spec, P(), P(), P(), P(), P()),
        out_specs=(
            token_spec,
            token_spec,
            P(None, "ens", None, None),
            P(None, "ens", None, None),
            P("ens"),
        ),
        check_vma=False,
    )
```

```python
import math

import jax
import jax.numpy as jnp
from jax import lax
from jax.sharding import Mesh
from jax.sharding import PartitionSpec as P

eps_norm = 1e-05
gelu_coef = 0.044715
GROUP = 8


def rounded(value):
    return lax.optimization_barrier(value.astype(jnp.bfloat16))


def gelu_value(value):
    factor = math.sqrt(2.0 / math.pi)
    return 0.5 * value * (1.0 + jnp.tanh(factor * (value + gelu_coef * value * value * value)))


def gelu_slope(value):
    factor = math.sqrt(2.0 / math.pi)
    tangent = jnp.tanh(factor * (value + gelu_coef * value * value * value))
    return 0.5 * (1.0 + tangent) + 0.5 * value * (1.0 - tangent * tangent) * factor * (
        1.0 + 3.0 * gelu_coef * value * value
    )


def table_parts(table):
    leading = table.astype(jnp.bfloat16)
    remainder = (table - leading.astype(jnp.float32)).astype(jnp.bfloat16)
    return (leading, remainder)


def data_table(form, data, parts):
    return jnp.einsum(form, data, parts[0], preferred_element_type=jnp.float32) + jnp.einsum(
        form, data, parts[1], preferred_element_type=jnp.float32
    )


def table_data(form, parts, data):
    return jnp.einsum(form, parts[0], data, preferred_element_type=jnp.float32) + jnp.einsum(
        form, parts[1], data, preferred_element_type=jnp.float32
    )


def longitude_tables(length, weights):
    places = jnp.arange(length, dtype=jnp.int32)
    numbers = jnp.arange(length // 2, dtype=jnp.int32)
    product = places[:, None] * numbers[None, :] % length
    angle = product.astype(jnp.float32) * (2.0 * math.pi / length)
    return (
        table_parts(jnp.cos(angle) * weights[None, :]),
        table_parts(jnp.sin(angle) * weights[None, :]),
    )


def latitude_tables(length):
    places = jnp.arange(length, dtype=jnp.int32)
    product = places[:, None] * places[None, :] % length
    angle = product.astype(jnp.float32) * (2.0 * math.pi / length)
    return (table_parts(jnp.cos(angle)), table_parts(jnp.sin(angle)))


def longitude_forward(field, cosine, sine, scale):
    real = data_table("nshwc,wk->nshkc", field, cosine) * scale
    imag = -data_table("nshwc,wk->nshkc", field, sine) * scale
    return (real, imag)


def longitude_inverse(real, imag, cosine, sine, scale):
    first = data_table("shkc,wk->shwc", real, cosine)
    second = data_table("shkc,wk->shwc", imag, sine)
    return (first - second) * scale


def latitude_forward(real, imag, cosine, sine):
    out_real = table_data("ah,nshkc->nsakc", cosine, real) + table_data("ah,nshkc->nsakc", sine, imag)
    out_imag = table_data("ah,nshkc->nsakc", cosine, imag) - table_data("ah,nshkc->nsakc", sine, real)
    return (out_real, out_imag)


def latitude_inverse(real, imag, cosine, sine):
    out_real = table_data("ah,nsakc->nshkc", cosine, real) - table_data("ah,nsakc->nshkc", sine, imag)
    out_imag = table_data("ah,nsakc->nshkc", cosine, imag) + table_data("ah,nsakc->nshkc", sine, real)
    return (out_real, out_imag)


def product(rows, weight):
    return jnp.dot(rows, weight, preferred_element_type=jnp.float32)


def adjoint(rows, weight):
    return lax.dot_general(rows, weight, (((1,), (1,)), ((), ())), preferred_element_type=jnp.float32)


def outer(left, right):
    return lax.dot_general(left, right, (((0,), (0,)), ((), ())), preferred_element_type=jnp.float32)


LON = ("lhi", "llo")


def body(tokens, cotangent, gain, weight_one, weight_two, bias_one, bias_two):
    field = tokens[0]
    cot_field = cotangent[0]
    samples, latitudes, local_width, width = field.shape
    lon_count = lax.axis_size(LON)
    group = lax.axis_size("llo")
    member_count = lax.axis_size("ens")
    full_width = local_width * lon_count
    modes = full_width // 2
    blocks = weight_one.shape[1]
    block_size = weight_one.shape[2]
    group_modes = modes // group
    block = lax.axis_index("lhi")
    member = lax.axis_index("ens")
    scale = 1.0 / math.sqrt(latitudes * full_width)
    full_weights = jnp.where(jnp.arange(modes) == 0, 1.0, 2.0).astype(jnp.float32)
    unit_weights = jnp.ones((modes,), jnp.float32)
    lon_cosine, lon_sine = longitude_tables(full_width, unit_weights)
    wide_cosine, wide_sine = longitude_tables(full_width, full_weights)
    lat_cosine, lat_sine = latitude_tables(latitudes)

    w1 = lax.dynamic_index_in_dim(weight_one, block, 1, keepdims=False)
    w2 = lax.dynamic_index_in_dim(weight_two, block, 1, keepdims=False)
    b1 = lax.dynamic_slice_in_dim(bias_one, block * block_size, block_size, 1)
    b2 = lax.dynamic_slice_in_dim(bias_two, block * block_size, block_size, 1)

    values = field.astype(jnp.float32)
    center = values - jnp.mean(values, axis=-1, keepdims=True)
    inv_dev = lax.rsqrt(jnp.mean(center * center, axis=-1, keepdims=True) + eps_norm)
    standard = center * inv_dev
    normed = (standard * gain).astype(jnp.bfloat16)

    both = jnp.stack([normed, cot_field])
    cols = lax.all_to_all(both, LON, split_axis=4, concat_axis=3, tiled=True)
    part_real, part_imag = longitude_forward(cols, lon_cosine, lon_sine, scale)
    part_real = rounded(part_real)
    part_imag = rounded(part_imag)
    exchanged = jnp.stack([part_real[0], part_imag[0], part_real[1], part_imag[1]])
    local = lax.all_to_all(exchanged, "llo", split_axis=3, concat_axis=4, tiled=True)
    local_shape = local.shape[1:]
    spec_real, spec_imag = latitude_forward(local[0::2], local[1::2], lat_cosine, lat_sine)
    position = lax.axis_index("llo")
    kw_local = lax.dynamic_slice_in_dim(full_weights, position * group_modes, group_modes, 0)
    kw_weights = kw_local[None, None, :, None]
    rows_real = rounded(spec_real[0]).reshape(-1, block_size)
    rows_imag = rounded(spec_imag[0]).reshape(-1, block_size)
    rows_filt_real = rounded(spec_real[1] * kw_weights).reshape(-1, block_size)
    rows_filt_imag = rounded(spec_imag[1] * kw_weights).reshape(-1, block_size)

    before_real = product(rows_real, w1[0]) - product(rows_imag, w1[1]) + b1[0]
    before_imag = product(rows_imag, w1[0]) + product(rows_real, w1[1]) + b1[1]
    hidden_real = gelu_value(before_real).astype(jnp.bfloat16)
    hidden_imag = gelu_value(before_imag).astype(jnp.bfloat16)
    filtered_real = (product(hidden_real, w2[0]) - product(hidden_imag, w2[1]) + b2[0]).astype(
        jnp.bfloat16
    )
    filtered_imag = (product(hidden_imag, w2[0]) + product(hidden_real, w2[1]) + b2[1]).astype(
        jnp.bfloat16
    )

    grad_hid_real = adjoint(rows_filt_real, w2[0]) + adjoint(rows_filt_imag, w2[1])
    grad_hid_imag = adjoint(rows_filt_imag, w2[0]) - adjoint(rows_filt_real, w2[1])
    grad_before_real = (grad_hid_real * gelu_slope(before_real)).astype(jnp.bfloat16)
    grad_before_imag = (grad_hid_imag * gelu_slope(before_imag)).astype(jnp.bfloat16)
    grad_spec_real = (
        adjoint(grad_before_real, w1[0]) + adjoint(grad_before_imag, w1[1])
    ).astype(jnp.bfloat16)
    grad_spec_imag = (
        adjoint(grad_before_imag, w1[0]) - adjoint(grad_before_real, w1[1])
    ).astype(jnp.bfloat16)
    second = jnp.stack(
        [
            outer(hidden_real, rows_filt_real) + outer(hidden_imag, rows_filt_imag),
            outer(hidden_real, rows_filt_imag) - outer(hidden_imag, rows_filt_real),
        ]
    )
    first = jnp.stack(
        [
            outer(rows_real, grad_before_real) + outer(rows_imag, grad_before_imag),
            outer(rows_real, grad_before_imag) - outer(rows_imag, grad_before_real),
        ]
    )

    back_in_real = jnp.stack([filtered_real, grad_spec_real]).reshape((2,) + local_shape)
    back_in_imag = jnp.stack([filtered_imag, grad_spec_imag]).reshape((2,) + local_shape)
    back_real, back_imag = latitude_inverse(back_in_real, back_in_imag, lat_cosine, lat_sine)
    back_stack = jnp.stack([back_real[0], back_imag[0], back_real[1], back_imag[1]]).astype(jnp.bfloat16)
    moved = lax.all_to_all(back_stack, "llo", split_axis=4, concat_axis=3, tiled=True)
    back_real = moved[0::2]
    back_imag = moved[1::2]
    spatial = longitude_inverse(back_real[0], back_imag[0], wide_cosine, wide_sine, scale)
    grad_spatial = longitude_inverse(back_real[1], back_imag[1], lon_cosine, lon_sine, scale)
    out_stack = jnp.stack([spatial.astype(jnp.bfloat16), grad_spatial.astype(jnp.bfloat16)])
    out_tokens = lax.all_to_all(out_stack, LON, split_axis=3, concat_axis=4, tiled=True)
    spatial_tokens = out_tokens[0]
    grad_field = out_tokens[1]

    mixed = (spatial_tokens.astype(jnp.float32) + normed.astype(jnp.float32)).astype(jnp.bfloat16)
    grad_normed = cot_field.astype(jnp.float32) + grad_field.astype(jnp.float32)
    gain_row = jnp.sum(grad_normed * standard, axis=(0, 1, 2))
    grad_hat = grad_normed * gain
    grad_in = inv_dev * (
        grad_hat
        - jnp.mean(grad_hat, axis=-1, keepdims=True)
        - standard * jnp.mean(grad_hat * standard, axis=-1, keepdims=True)
    )

    share = blocks // member_count
    gain_share = width // member_count
    row_factor = 1.0 / math.sqrt(member_count * samples * latitudes * modes)
    token_factor = 1.0 / math.sqrt(member_count * samples * latitudes * full_width)
    pieces = group * member_count
    weight_size = 2 * 2 * block_size * block_size
    weight_piece = weight_size // pieces
    payload = jnp.concatenate([first.reshape(-1), second.reshape(-1)]).reshape(
        group, member_count, weight_piece
    )
    summed = jnp.sum(lax.all_to_all(payload, "llo", split_axis=0, concat_axis=0, tiled=True), axis=0)
    summed = jnp.sum(lax.all_to_all(summed, "ens", split_axis=0, concat_axis=0, tiled=True), axis=0)
    dest_member = jnp.arange(member_count * blocks)[:, None] // blocks
    keep = (dest_member == block // share).astype(jnp.float32)
    routed = lax.all_to_all(keep * summed[None, :], ("ens", "lhi"), split_axis=0, concat_axis=0, tiled=True)
    routed = routed.reshape(member_count, blocks, weight_piece)
    mine = lax.dynamic_slice_in_dim(routed, member * share, share, 1)
    local_result = mine.reshape(member_count, share * weight_piece)
    spread = jnp.broadcast_to(local_result[None], (group,) + local_result.shape)
    spread = lax.all_to_all(spread, "llo", split_axis=0, concat_axis=0, tiled=True)
    weights_all = spread.reshape(group, member_count, share, weight_piece)
    weights_all = jnp.transpose(weights_all, (2, 0, 1, 3)).reshape(share, 2, 2, block_size, block_size)
    sum_first = jnp.transpose(weights_all[:, 0], (1, 0, 2, 3))
    sum_second = jnp.transpose(weights_all[:, 1], (1, 0, 2, 3))

    devices = member_count * lon_count
    gain_rows = jnp.broadcast_to(
        gain_row.reshape(member_count, 1, gain_share), (member_count, devices // member_count, gain_share)
    ).reshape(devices, gain_share)
    gain_rows = lax.all_to_all(gain_rows, ("ens", "lhi", "llo"), split_axis=0, concat_axis=0, tiled=True)
    sum_gain = jnp.sum(gain_rows, axis=0)
    return (
        mixed[None],
        grad_in.astype(jnp.bfloat16)[None],
        sum_first * row_factor,
        sum_second * row_factor,
        sum_gain * token_factor,
    )


def solution(mesh):
    ens_size, lon_size = mesh.devices.shape
    view = Mesh(
        mesh.devices.reshape(ens_size, lon_size // GROUP, GROUP), ("ens", "lhi", "llo")
    )
    token_spec = P("ens", None, None, LON, None)
    return jax.shard_map(
        body,
        mesh=view,
        in_specs=(token_spec, token_spec, P(), P(), P(), P(), P()),
        out_specs=(
            token_spec,
            token_spec,
            P(None, "ens", None, None),
            P(None, "ens", None, None),
            P("ens"),
        ),
        check_vma=False,
    )
```

```python
import math

import jax
import jax.numpy as jnp
from jax import lax
from jax.sharding import Mesh
from jax.sharding import PartitionSpec as P

eps_norm = 1e-05
gelu_coef = 0.044715
GROUP = 8


def rounded(value):
    return lax.optimization_barrier(value.astype(jnp.bfloat16))


def gelu_value(value):
    factor = math.sqrt(2.0 / math.pi)
    return 0.5 * value * (1.0 + jnp.tanh(factor * (value + gelu_coef * value * value * value)))


def gelu_slope(value):
    factor = math.sqrt(2.0 / math.pi)
    tangent = jnp.tanh(factor * (value + gelu_coef * value * value * value))
    return 0.5 * (1.0 + tangent) + 0.5 * value * (1.0 - tangent * tangent) * factor * (
        1.0 + 3.0 * gelu_coef * value * value
    )


def table_parts(table):
    leading = table.astype(jnp.bfloat16)
    remainder = (table - leading.astype(jnp.float32)).astype(jnp.bfloat16)
    return (leading, remainder)


def data_table(form, data, parts):
    return jnp.einsum(form, data, parts[0], preferred_element_type=jnp.float32) + jnp.einsum(
        form, data, parts[1], preferred_element_type=jnp.float32
    )


def table_data(form, parts, data):
    return jnp.einsum(form, parts[0], data, preferred_element_type=jnp.float32) + jnp.einsum(
        form, parts[1], data, preferred_element_type=jnp.float32
    )


def longitude_tables(length, weights):
    places = jnp.arange(length, dtype=jnp.int32)
    numbers = jnp.arange(length // 2, dtype=jnp.int32)
    product = places[:, None] * numbers[None, :] % length
    angle = product.astype(jnp.float32) * (2.0 * math.pi / length)
    return (
        table_parts(jnp.cos(angle) * weights[None, :]),
        table_parts(jnp.sin(angle) * weights[None, :]),
    )


def latitude_tables(length):
    places = jnp.arange(length, dtype=jnp.int32)
    product = places[:, None] * places[None, :] % length
    angle = product.astype(jnp.float32) * (2.0 * math.pi / length)
    return (table_parts(jnp.cos(angle)), table_parts(jnp.sin(angle)))


def longitude_forward(field, cosine, sine, scale):
    real = data_table("nshwc,wk->nshkc", field, cosine) * scale
    imag = -data_table("nshwc,wk->nshkc", field, sine) * scale
    return (real, imag)


def longitude_inverse(real, imag, cosine, sine, scale):
    first = data_table("shkc,wk->shwc", real, cosine)
    second = data_table("shkc,wk->shwc", imag, sine)
    return (first - second) * scale


def latitude_forward(real, imag, cosine, sine):
    out_real = table_data("ah,nshkc->nsakc", cosine, real) + table_data("ah,nshkc->nsakc", sine, imag)
    out_imag = table_data("ah,nshkc->nsakc", cosine, imag) - table_data("ah,nshkc->nsakc", sine, real)
    return (out_real, out_imag)


def latitude_inverse(real, imag, cosine, sine):
    out_real = table_data("ah,nsakc->nshkc", cosine, real) - table_data("ah,nsakc->nshkc", sine, imag)
    out_imag = table_data("ah,nsakc->nshkc", cosine, imag) + table_data("ah,nsakc->nshkc", sine, real)
    return (out_real, out_imag)


def product(rows, weight):
    return jnp.dot(rows, weight, preferred_element_type=jnp.float32)


def adjoint(rows, weight):
    return lax.dot_general(rows, weight, (((1,), (1,)), ((), ())), preferred_element_type=jnp.float32)


def outer(left, right):
    return lax.dot_general(left, right, (((0,), (0,)), ((), ())), preferred_element_type=jnp.float32)


LON = ("lhi", "llo")


def body(tokens, cotangent, gain, weight_one, weight_two, bias_one, bias_two):
    field = tokens[0]
    cot_field = cotangent[0]
    samples, latitudes, local_width, width = field.shape
    lon_count = lax.axis_size(LON)
    group = lax.axis_size("llo")
    member_count = lax.axis_size("ens")
    full_width = local_width * lon_count
    modes = full_width // 2
    blocks = weight_one.shape[1]
    block_size = weight_one.shape[2]
    group_modes = modes // group
    block = lax.axis_index("lhi")
    member = lax.axis_index("ens")
    scale = 1.0 / math.sqrt(latitudes * full_width)
    full_weights = jnp.where(jnp.arange(modes) == 0, 1.0, 2.0).astype(jnp.float32)
    unit_weights = jnp.ones((modes,), jnp.float32)
    lon_cosine, lon_sine = longitude_tables(full_width, unit_weights)
    wide_cosine, wide_sine = longitude_tables(full_width, full_weights)
    lat_cosine, lat_sine = latitude_tables(latitudes)

    w1 = lax.dynamic_index_in_dim(weight_one, block, 1, keepdims=False)
    w2 = lax.dynamic_index_in_dim(weight_two, block, 1, keepdims=False)
    b1 = lax.dynamic_slice_in_dim(bias_one, block * block_size, block_size, 1)
    b2 = lax.dynamic_slice_in_dim(bias_two, block * block_size, block_size, 1)

    values = field.astype(jnp.float32)
    center = values - jnp.mean(values, axis=-1, keepdims=True)
    inv_dev = lax.rsqrt(jnp.mean(center * center, axis=-1, keepdims=True) + eps_norm)
    standard = center * inv_dev
    normed = (standard * gain).astype(jnp.bfloat16)

    both = jnp.stack([normed, cot_field])
    cols = lax.all_to_all(both, LON, split_axis=4, concat_axis=3, tiled=True)
    forward_table = jnp.concatenate([lon_cosine[0], lon_cosine[1], lon_sine[0], lon_sine[1]], axis=1)
    spectra = jnp.einsum("nshwc,wm->nshmc", cols, forward_table, preferred_element_type=jnp.float32)
    part_real = rounded((spectra[:, :, :, :modes] + spectra[:, :, :, modes : 2 * modes]) * scale)
    part_imag = rounded(-(spectra[:, :, :, 2 * modes : 3 * modes] + spectra[:, :, :, 3 * modes :]) * scale)
    exchanged = jnp.stack([part_real[0], part_imag[0], part_real[1], part_imag[1]])
    local = lax.all_to_all(exchanged, "llo", split_axis=3, concat_axis=4, tiled=True)
    local_shape = local.shape[1:]
    cos_lead, cos_rest = lat_cosine
    sin_lead, sin_rest = lat_sine
    from_real = jnp.stack([cos_lead, cos_rest, -sin_lead, -sin_rest])
    from_imag = jnp.stack([sin_lead, sin_rest, cos_lead, cos_rest])
    lat_form = "qah,nshkc->qnsakc"
    spec = jnp.einsum(lat_form, from_real, local[0::2], preferred_element_type=jnp.float32) + jnp.einsum(
        lat_form, from_imag, local[1::2], preferred_element_type=jnp.float32
    )
    spec = jnp.stack([spec[0] + spec[1], spec[2] + spec[3]], axis=-2)
    position = lax.axis_index("llo")
    kw_local = lax.dynamic_slice_in_dim(full_weights, position * group_modes, group_modes, 0)
    kw_scale = jnp.stack([jnp.ones_like(kw_local), kw_local])[:, None, None, :, None, None]
    rows_all = rounded(spec * kw_scale).reshape(2, -1, 2 * block_size)
    rows_spec = rows_all[0]
    rows_grad = rows_all[1]

    def complex_matrix(weight):
        top = jnp.concatenate([weight[0], weight[1]], axis=1)
        bottom = jnp.concatenate([-weight[1], weight[0]], axis=1)
        return jnp.concatenate([top, bottom], axis=0)

    m1 = complex_matrix(w1)
    m2 = complex_matrix(w2)
    bias_first = jnp.concatenate([b1[0], b1[1]])
    bias_second = jnp.concatenate([b2[0], b2[1]])
    before = product(rows_spec, m1) + bias_first
    hidden = gelu_value(before).astype(jnp.bfloat16)
    filtered = (product(hidden, m2) + bias_second).astype(jnp.bfloat16)
    grad_hidden = adjoint(rows_grad, m2)
    grad_before = (grad_hidden * gelu_slope(before)).astype(jnp.bfloat16)
    grad_spec = adjoint(grad_before, m1).astype(jnp.bfloat16)

    def fold(full):
        return jnp.stack(
            [
                full[:block_size, :block_size] + full[block_size:, block_size:],
                full[:block_size, block_size:] - full[block_size:, :block_size],
            ]
        )

    second = fold(outer(hidden, rows_grad))
    first = fold(outer(rows_spec, grad_before))

    back_in = jnp.stack([filtered, grad_spec]).reshape(spec.shape)
    to_real = jnp.stack([cos_lead, cos_rest, sin_lead, sin_rest])
    to_imag = jnp.stack([-sin_lead, -sin_rest, cos_lead, cos_rest])
    inv_form = "qah,nsakc->qnshkc"
    back = jnp.einsum(inv_form, to_real, back_in[:, :, :, :, 0], preferred_element_type=jnp.float32) + jnp.einsum(
        inv_form, to_imag, back_in[:, :, :, :, 1], preferred_element_type=jnp.float32
    )
    back_real = back[0] + back[1]
    back_imag = back[2] + back[3]
    back_stack = jnp.stack([back_real[0], back_imag[0], back_real[1], back_imag[1]]).astype(jnp.bfloat16)
    moved = lax.all_to_all(back_stack, "llo", split_axis=4, concat_axis=3, tiled=True)
    back_real = moved[0::2]
    back_imag = moved[1::2]
    spatial = longitude_inverse(back_real[0], back_imag[0], wide_cosine, wide_sine, scale)
    grad_spatial = longitude_inverse(back_real[1], back_imag[1], lon_cosine, lon_sine, scale)
    out_stack = jnp.stack([spatial.astype(jnp.bfloat16), grad_spatial.astype(jnp.bfloat16)])
    out_tokens = lax.all_to_all(out_stack, LON, split_axis=3, concat_axis=4, tiled=True)
    spatial_tokens = out_tokens[0]
    grad_field = out_tokens[1]

    mixed = (spatial_tokens.astype(jnp.float32) + normed.astype(jnp.float32)).astype(jnp.bfloat16)
    grad_normed = cot_field.astype(jnp.float32) + grad_field.astype(jnp.float32)
    gain_row = jnp.sum(grad_normed * standard, axis=(0, 1, 2))
    grad_hat = grad_normed * gain
    grad_in = inv_dev * (
        grad_hat
        - jnp.mean(grad_hat, axis=-1, keepdims=True)
        - standard * jnp.mean(grad_hat * standard, axis=-1, keepdims=True)
    )

    share = blocks // member_count
    gain_share = width // member_count
    row_factor = 1.0 / math.sqrt(member_count * samples * latitudes * modes)
    token_factor = 1.0 / math.sqrt(member_count * samples * latitudes * full_width)
    pieces = group * member_count
    weight_size = 2 * 2 * block_size * block_size
    weight_piece = weight_size // pieces
    payload = jnp.concatenate([first.reshape(-1), second.reshape(-1)]).reshape(
        group, member_count, weight_piece
    )
    summed = jnp.sum(lax.all_to_all(payload, "llo", split_axis=0, concat_axis=0, tiled=True), axis=0)
    summed = jnp.sum(lax.all_to_all(summed, "ens", split_axis=0, concat_axis=0, tiled=True), axis=0)
    dest_member = jnp.arange(member_count * blocks)[:, None] // blocks
    keep = (dest_member == block // share).astype(jnp.float32)
    routed = lax.all_to_all(keep * summed[None, :], ("ens", "lhi"), split_axis=0, concat_axis=0, tiled=True)
    routed = routed.reshape(member_count, blocks, weight_piece)
    mine = lax.dynamic_slice_in_dim(routed, member * share, share, 1)
    local_result = mine.reshape(member_count, share * weight_piece)
    spread = jnp.broadcast_to(local_result[None], (group,) + local_result.shape)
    spread = lax.all_to_all(spread, "llo", split_axis=0, concat_axis=0, tiled=True)
    weights_all = spread.reshape(group, member_count, share, weight_piece)
    weights_all = jnp.transpose(weights_all, (2, 0, 1, 3)).reshape(share, 2, 2, block_size, block_size)
    sum_first = jnp.transpose(weights_all[:, 0], (1, 0, 2, 3))
    sum_second = jnp.transpose(weights_all[:, 1], (1, 0, 2, 3))

    devices = member_count * lon_count
    gain_rows = jnp.broadcast_to(
        gain_row.reshape(member_count, 1, gain_share), (member_count, devices // member_count, gain_share)
    ).reshape(devices, gain_share)
    gain_rows = lax.all_to_all(gain_rows, ("ens", "lhi", "llo"), split_axis=0, concat_axis=0, tiled=True)
    sum_gain = jnp.sum(gain_rows, axis=0)
    return (
        mixed[None],
        grad_in.astype(jnp.bfloat16)[None],
        sum_first * row_factor,
        sum_second * row_factor,
        sum_gain * token_factor,
    )


def solution(mesh):
    ens_size, lon_size = mesh.devices.shape
    view = Mesh(
        mesh.devices.reshape(ens_size, lon_size // GROUP, GROUP), ("ens", "lhi", "llo")
    )
    token_spec = P("ens", None, None, LON, None)
    return jax.shard_map(
        body,
        mesh=view,
        in_specs=(token_spec, token_spec, P(), P(), P(), P(), P()),
        out_specs=(
            token_spec,
            token_spec,
            P(None, "ens", None, None),
            P(None, "ens", None, None),
            P("ens"),
        ),
        check_vma=False,
    )
```

```python
import math

import jax
import jax.numpy as jnp
from jax import lax
from jax.sharding import Mesh
from jax.sharding import PartitionSpec as P

eps_norm = 1e-05
gelu_coef = 0.044715
GROUP = 8


def rounded(value):
    return lax.optimization_barrier(value.astype(jnp.bfloat16))


def gelu_value(value):
    factor = math.sqrt(2.0 / math.pi)
    return 0.5 * value * (1.0 + jnp.tanh(factor * (value + gelu_coef * value * value * value)))


def gelu_slope(value):
    factor = math.sqrt(2.0 / math.pi)
    tangent = jnp.tanh(factor * (value + gelu_coef * value * value * value))
    return 0.5 * (1.0 + tangent) + 0.5 * value * (1.0 - tangent * tangent) * factor * (
        1.0 + 3.0 * gelu_coef * value * value
    )


def table_parts(table):
    leading = table.astype(jnp.bfloat16)
    remainder = (table - leading.astype(jnp.float32)).astype(jnp.bfloat16)
    return (leading, remainder)


def data_table(form, data, parts):
    return jnp.einsum(form, data, parts[0], preferred_element_type=jnp.float32) + jnp.einsum(
        form, data, parts[1], preferred_element_type=jnp.float32
    )


def table_data(form, parts, data):
    return jnp.einsum(form, parts[0], data, preferred_element_type=jnp.float32) + jnp.einsum(
        form, parts[1], data, preferred_element_type=jnp.float32
    )


def longitude_tables(length, weights):
    places = jnp.arange(length, dtype=jnp.int32)
    numbers = jnp.arange(length // 2, dtype=jnp.int32)
    product = places[:, None] * numbers[None, :] % length
    angle = product.astype(jnp.float32) * (2.0 * math.pi / length)
    return (
        table_parts(jnp.cos(angle) * weights[None, :]),
        table_parts(jnp.sin(angle) * weights[None, :]),
    )


def latitude_tables(length):
    places = jnp.arange(length, dtype=jnp.int32)
    product = places[:, None] * places[None, :] % length
    angle = product.astype(jnp.float32) * (2.0 * math.pi / length)
    return (table_parts(jnp.cos(angle)), table_parts(jnp.sin(angle)))


def longitude_forward(field, cosine, sine, scale):
    real = data_table("nshwc,wk->nshkc", field, cosine) * scale
    imag = -data_table("nshwc,wk->nshkc", field, sine) * scale
    return (real, imag)


def longitude_inverse(real, imag, cosine, sine, scale):
    first = data_table("shkc,wk->shwc", real, cosine)
    second = data_table("shkc,wk->shwc", imag, sine)
    return (first - second) * scale


def latitude_forward(real, imag, cosine, sine):
    out_real = table_data("ah,nshkc->nsakc", cosine, real) + table_data("ah,nshkc->nsakc", sine, imag)
    out_imag = table_data("ah,nshkc->nsakc", cosine, imag) - table_data("ah,nshkc->nsakc", sine, real)
    return (out_real, out_imag)


def latitude_inverse(real, imag, cosine, sine):
    out_real = table_data("ah,nsakc->nshkc", cosine, real) - table_data("ah,nsakc->nshkc", sine, imag)
    out_imag = table_data("ah,nsakc->nshkc", cosine, imag) + table_data("ah,nsakc->nshkc", sine, real)
    return (out_real, out_imag)


def product(rows, weight):
    return jnp.dot(rows, weight, preferred_element_type=jnp.float32)


def adjoint(rows, weight):
    return lax.dot_general(rows, weight, (((1,), (1,)), ((), ())), preferred_element_type=jnp.float32)


def outer(left, right):
    return lax.dot_general(left, right, (((0,), (0,)), ((), ())), preferred_element_type=jnp.float32)


LON = ("lhi", "llo")


def body(tokens, cotangent, gain, weight_one, weight_two, bias_one, bias_two):
    field = tokens[0]
    cot_field = cotangent[0]
    samples, latitudes, local_width, width = field.shape
    lon_count = lax.axis_size(LON)
    group = lax.axis_size("llo")
    member_count = lax.axis_size("ens")
    full_width = local_width * lon_count
    modes = full_width // 2
    blocks = weight_one.shape[1]
    block_size = weight_one.shape[2]
    group_modes = modes // group
    block = lax.axis_index("lhi")
    member = lax.axis_index("ens")
    scale = 1.0 / math.sqrt(latitudes * full_width)
    full_weights = jnp.where(jnp.arange(modes) == 0, 1.0, 2.0).astype(jnp.float32)
    unit_weights = jnp.ones((modes,), jnp.float32)
    lon_cosine, lon_sine = longitude_tables(full_width, unit_weights)
    wide_cosine, wide_sine = longitude_tables(full_width, full_weights)
    lat_cosine, lat_sine = latitude_tables(latitudes)

    w1 = lax.dynamic_index_in_dim(weight_one, block, 1, keepdims=False)
    w2 = lax.dynamic_index_in_dim(weight_two, block, 1, keepdims=False)
    b1 = lax.dynamic_slice_in_dim(bias_one, block * block_size, block_size, 1)
    b2 = lax.dynamic_slice_in_dim(bias_two, block * block_size, block_size, 1)

    values = field.astype(jnp.float32)
    center = values - jnp.mean(values, axis=-1, keepdims=True)
    inv_dev = lax.rsqrt(jnp.mean(center * center, axis=-1, keepdims=True) + eps_norm)
    standard = center * inv_dev
    normed = (standard * gain).astype(jnp.bfloat16)

    both = jnp.stack([normed, cot_field])
    cols = lax.all_to_all(both, LON, split_axis=4, concat_axis=3, tiled=True)
    forward_table = jnp.concatenate([lon_cosine[0], lon_cosine[1], lon_sine[0], lon_sine[1]], axis=1)
    spectra = jnp.einsum("nshwc,wm->nshmc", cols, forward_table, preferred_element_type=jnp.float32)
    part_real = rounded((spectra[:, :, :, :modes] + spectra[:, :, :, modes : 2 * modes]) * scale)
    part_imag = rounded(-(spectra[:, :, :, 2 * modes : 3 * modes] + spectra[:, :, :, 3 * modes :]) * scale)
    exchanged = jnp.stack([part_real[0], part_imag[0], part_real[1], part_imag[1]])
    local = lax.all_to_all(exchanged, "llo", split_axis=3, concat_axis=4, tiled=True)
    local_shape = local.shape[1:]
    cos_lead, cos_rest = lat_cosine
    sin_lead, sin_rest = lat_sine
    from_real = jnp.stack([cos_lead, cos_rest, -sin_lead, -sin_rest])
    from_imag = jnp.stack([sin_lead, sin_rest, cos_lead, cos_rest])
    lat_form = "qah,nshkc->qnsakc"
    spec = jnp.einsum(lat_form, from_real, local[0::2], preferred_element_type=jnp.float32) + jnp.einsum(
        lat_form, from_imag, local[1::2], preferred_element_type=jnp.float32
    )
    spec = jnp.stack([spec[0] + spec[1], spec[2] + spec[3]], axis=-2)
    position = lax.axis_index("llo")
    kw_local = lax.dynamic_slice_in_dim(full_weights, position * group_modes, group_modes, 0)
    kw_scale = jnp.stack([jnp.ones_like(kw_local), kw_local])[:, None, None, :, None, None]
    rows_all = rounded(spec * kw_scale).reshape(2, -1, 2 * block_size)
    rows_spec = rows_all[0]
    rows_grad = rows_all[1]

    def complex_matrix(weight):
        top = jnp.concatenate([weight[0], weight[1]], axis=1)
        bottom = jnp.concatenate([-weight[1], weight[0]], axis=1)
        return jnp.concatenate([top, bottom], axis=0)

    m1 = complex_matrix(w1)
    m2 = complex_matrix(w2)
    bias_first = jnp.concatenate([b1[0], b1[1]])
    bias_second = jnp.concatenate([b2[0], b2[1]])
    before = product(rows_spec, m1) + bias_first
    hidden = gelu_value(before).astype(jnp.bfloat16)
    filtered = (product(hidden, m2) + bias_second).astype(jnp.bfloat16)
    grad_hidden = adjoint(rows_grad, m2)
    grad_before = (grad_hidden * gelu_slope(before)).astype(jnp.bfloat16)
    grad_spec = adjoint(grad_before, m1).astype(jnp.bfloat16)

    def fold(full):
        return jnp.stack(
            [
                full[:block_size, :block_size] + full[block_size:, block_size:],
                full[:block_size, block_size:] - full[block_size:, :block_size],
            ]
        )

    second = fold(outer(hidden, rows_grad))
    first = fold(outer(rows_spec, grad_before))

    back_in = jnp.stack([filtered, grad_spec]).reshape(spec.shape)
    to_real = jnp.stack([cos_lead, cos_rest, sin_lead, sin_rest])
    to_imag = jnp.stack([-sin_lead, -sin_rest, cos_lead, cos_rest])
    inv_form = "qah,nsakc->qnshkc"
    back = jnp.einsum(inv_form, to_real, back_in[:, :, :, :, 0], preferred_element_type=jnp.float32) + jnp.einsum(
        inv_form, to_imag, back_in[:, :, :, :, 1], preferred_element_type=jnp.float32
    )
    back_real = back[0] + back[1]
    back_imag = back[2] + back[3]
    back_stack = jnp.stack([back_real[0], back_imag[0], back_real[1], back_imag[1]]).astype(jnp.bfloat16)
    moved = lax.all_to_all(back_stack, "llo", split_axis=4, concat_axis=3, tiled=True)
    back_real = moved[0::2]
    back_imag = moved[1::2]
    spatial = longitude_inverse(back_real[0], back_imag[0], wide_cosine, wide_sine, scale)
    grad_spatial = longitude_inverse(back_real[1], back_imag[1], lon_cosine, lon_sine, scale)
    out_stack = jnp.stack([spatial.astype(jnp.bfloat16), grad_spatial.astype(jnp.bfloat16)])
    out_tokens = lax.all_to_all(out_stack, LON, split_axis=3, concat_axis=4, tiled=True)
    spatial_tokens = out_tokens[0]
    grad_field = out_tokens[1]

    mixed = (spatial_tokens.astype(jnp.float32) + normed.astype(jnp.float32)).astype(jnp.bfloat16)
    grad_normed = cot_field.astype(jnp.float32) + grad_field.astype(jnp.float32)
    gain_row = jnp.sum(grad_normed * standard, axis=(0, 1, 2))
    grad_hat = grad_normed * gain
    grad_in = inv_dev * (
        grad_hat
        - jnp.mean(grad_hat, axis=-1, keepdims=True)
        - standard * jnp.mean(grad_hat * standard, axis=-1, keepdims=True)
    )

    share = blocks // member_count
    gain_share = width // member_count
    row_factor = 1.0 / math.sqrt(member_count * samples * latitudes * modes)
    token_factor = 1.0 / math.sqrt(member_count * samples * latitudes * full_width)
    pieces = group * member_count
    weight_size = 2 * 2 * block_size * block_size
    weight_piece = weight_size // pieces
    payload = jnp.concatenate([first.reshape(-1), second.reshape(-1)]).reshape(
        group, member_count, weight_piece
    )
    payload = jnp.transpose(payload, (1, 0, 2)).reshape(pieces, weight_piece)
    summed = jnp.sum(lax.all_to_all(payload, ("ens", "llo"), split_axis=0, concat_axis=0, tiled=True), axis=0)
    dest_member = jnp.arange(member_count * blocks)[:, None] // blocks
    keep = (dest_member == block // share).astype(jnp.float32)
    routed = lax.all_to_all(keep * summed[None, :], ("ens", "lhi"), split_axis=0, concat_axis=0, tiled=True)
    routed = routed.reshape(member_count, blocks, weight_piece)
    mine = lax.dynamic_slice_in_dim(routed, member * share, share, 1)
    local_result = mine.reshape(member_count, share * weight_piece)
    spread = jnp.broadcast_to(local_result[None], (group,) + local_result.shape)
    spread = lax.all_to_all(spread, "llo", split_axis=0, concat_axis=0, tiled=True)
    weights_all = spread.reshape(group, member_count, share, weight_piece)
    weights_all = jnp.transpose(weights_all, (2, 0, 1, 3)).reshape(share, 2, 2, block_size, block_size)
    sum_first = jnp.transpose(weights_all[:, 0], (1, 0, 2, 3))
    sum_second = jnp.transpose(weights_all[:, 1], (1, 0, 2, 3))

    devices = member_count * lon_count
    gain_rows = jnp.broadcast_to(
        gain_row.reshape(member_count, 1, gain_share), (member_count, devices // member_count, gain_share)
    ).reshape(devices, gain_share)
    gain_rows = lax.all_to_all(gain_rows, ("ens", "lhi", "llo"), split_axis=0, concat_axis=0, tiled=True)
    sum_gain = jnp.sum(gain_rows, axis=0)
    return (
        mixed[None],
        grad_in.astype(jnp.bfloat16)[None],
        sum_first * row_factor,
        sum_second * row_factor,
        sum_gain * token_factor,
    )


def solution(mesh):
    ens_size, lon_size = mesh.devices.shape
    view = Mesh(
        mesh.devices.reshape(ens_size, lon_size // GROUP, GROUP), ("ens", "lhi", "llo")
    )
    token_spec = P("ens", None, None, LON, None)
    return jax.shard_map(
        body,
        mesh=view,
        in_specs=(token_spec, token_spec, P(), P(), P(), P(), P()),
        out_specs=(
            token_spec,
            token_spec,
            P(None, "ens", None, None),
            P(None, "ens", None, None),
            P("ens"),
        ),
        check_vma=False,
    )
```

```python
import math

import jax
import jax.numpy as jnp
from jax import lax
from jax.sharding import Mesh
from jax.sharding import PartitionSpec as P

eps_norm = 1e-05
gelu_coef = 0.044715
GROUP = 8


def rounded(value):
    return lax.optimization_barrier(value.astype(jnp.bfloat16))


def gelu_value(value):
    factor = math.sqrt(2.0 / math.pi)
    return 0.5 * value * (1.0 + jnp.tanh(factor * (value + gelu_coef * value * value * value)))


def gelu_slope(value):
    factor = math.sqrt(2.0 / math.pi)
    tangent = jnp.tanh(factor * (value + gelu_coef * value * value * value))
    return 0.5 * (1.0 + tangent) + 0.5 * value * (1.0 - tangent * tangent) * factor * (
        1.0 + 3.0 * gelu_coef * value * value
    )


def table_parts(table):
    leading = table.astype(jnp.bfloat16)
    remainder = (table - leading.astype(jnp.float32)).astype(jnp.bfloat16)
    return (leading, remainder)


def data_table(form, data, parts):
    return jnp.einsum(form, data, parts[0], preferred_element_type=jnp.float32) + jnp.einsum(
        form, data, parts[1], preferred_element_type=jnp.float32
    )


def table_data(form, parts, data):
    return jnp.einsum(form, parts[0], data, preferred_element_type=jnp.float32) + jnp.einsum(
        form, parts[1], data, preferred_element_type=jnp.float32
    )


def longitude_tables(length, weights):
    places = jnp.arange(length, dtype=jnp.int32)
    numbers = jnp.arange(length // 2, dtype=jnp.int32)
    product = places[:, None] * numbers[None, :] % length
    angle = product.astype(jnp.float32) * (2.0 * math.pi / length)
    return (
        table_parts(jnp.cos(angle) * weights[None, :]),
        table_parts(jnp.sin(angle) * weights[None, :]),
    )


def latitude_tables(length):
    places = jnp.arange(length, dtype=jnp.int32)
    product = places[:, None] * places[None, :] % length
    angle = product.astype(jnp.float32) * (2.0 * math.pi / length)
    return (table_parts(jnp.cos(angle)), table_parts(jnp.sin(angle)))


def longitude_forward(field, cosine, sine, scale):
    real = data_table("nshwc,wk->nshkc", field, cosine) * scale
    imag = -data_table("nshwc,wk->nshkc", field, sine) * scale
    return (real, imag)


def longitude_inverse(real, imag, cosine, sine, scale):
    first = data_table("shkc,wk->shwc", real, cosine)
    second = data_table("shkc,wk->shwc", imag, sine)
    return (first - second) * scale


def latitude_forward(real, imag, cosine, sine):
    out_real = table_data("ah,nshkc->nsakc", cosine, real) + table_data("ah,nshkc->nsakc", sine, imag)
    out_imag = table_data("ah,nshkc->nsakc", cosine, imag) - table_data("ah,nshkc->nsakc", sine, real)
    return (out_real, out_imag)


def latitude_inverse(real, imag, cosine, sine):
    out_real = table_data("ah,nsakc->nshkc", cosine, real) - table_data("ah,nsakc->nshkc", sine, imag)
    out_imag = table_data("ah,nsakc->nshkc", cosine, imag) + table_data("ah,nsakc->nshkc", sine, real)
    return (out_real, out_imag)


def product(rows, weight):
    return jnp.dot(rows, weight, preferred_element_type=jnp.float32)


def adjoint(rows, weight):
    return lax.dot_general(rows, weight, (((1,), (1,)), ((), ())), preferred_element_type=jnp.float32)


def outer(left, right):
    return lax.dot_general(left, right, (((0,), (0,)), ((), ())), preferred_element_type=jnp.float32)


LON = ("lhi", "llo")


def body(tokens, cotangent, gain, weight_one, weight_two, bias_one, bias_two):
    field = tokens[0]
    cot_field = cotangent[0]
    samples, latitudes, local_width, width = field.shape
    lon_count = lax.axis_size(LON)
    group = lax.axis_size("llo")
    member_count = lax.axis_size("ens")
    full_width = local_width * lon_count
    modes = full_width // 2
    blocks = weight_one.shape[1]
    block_size = weight_one.shape[2]
    group_modes = modes // group
    block = lax.axis_index("lhi")
    member = lax.axis_index("ens")
    scale = 1.0 / math.sqrt(latitudes * full_width)
    full_weights = jnp.where(jnp.arange(modes) == 0, 1.0, 2.0).astype(jnp.float32)
    unit_weights = jnp.ones((modes,), jnp.float32)
    lon_cosine, lon_sine = longitude_tables(full_width, unit_weights)
    wide_cosine, wide_sine = longitude_tables(full_width, full_weights)
    lat_cosine, lat_sine = latitude_tables(latitudes)

    w1 = lax.dynamic_index_in_dim(weight_one, block, 1, keepdims=False)
    w2 = lax.dynamic_index_in_dim(weight_two, block, 1, keepdims=False)
    b1 = lax.dynamic_slice_in_dim(bias_one, block * block_size, block_size, 1)
    b2 = lax.dynamic_slice_in_dim(bias_two, block * block_size, block_size, 1)

    values = field.astype(jnp.float32)
    center = values - jnp.mean(values, axis=-1, keepdims=True)
    inv_dev = lax.rsqrt(jnp.mean(center * center, axis=-1, keepdims=True) + eps_norm)
    standard = center * inv_dev
    normed = (standard * gain).astype(jnp.bfloat16)

    both = jnp.stack([normed, cot_field])
    cols = lax.all_to_all(both, LON, split_axis=4, concat_axis=3, tiled=True)
    forward_table = jnp.concatenate([lon_cosine[0], lon_cosine[1], lon_sine[0], lon_sine[1]], axis=1)
    spectra = jnp.einsum("nshwc,wm->nshmc", cols, forward_table, preferred_element_type=jnp.float32)
    part_real = rounded((spectra[:, :, :, :modes] + spectra[:, :, :, modes : 2 * modes]) * scale)
    part_imag = rounded(-(spectra[:, :, :, 2 * modes : 3 * modes] + spectra[:, :, :, 3 * modes :]) * scale)
    exchanged = jnp.stack([part_real[0], part_imag[0], part_real[1], part_imag[1]])
    local = lax.all_to_all(exchanged, "llo", split_axis=3, concat_axis=4, tiled=True)
    local_shape = local.shape[1:]
    cos_lead, cos_rest = lat_cosine
    sin_lead, sin_rest = lat_sine
    from_real = jnp.stack([cos_lead, cos_rest, -sin_lead, -sin_rest])
    from_imag = jnp.stack([sin_lead, sin_rest, cos_lead, cos_rest])
    lat_form = "qah,nshkc->qnsakc"
    spec = jnp.einsum(lat_form, from_real, local[0::2], preferred_element_type=jnp.float32) + jnp.einsum(
        lat_form, from_imag, local[1::2], preferred_element_type=jnp.float32
    )
    spec = jnp.stack([spec[0] + spec[1], spec[2] + spec[3]], axis=-2)
    position = lax.axis_index("llo")
    kw_local = lax.dynamic_slice_in_dim(full_weights, position * group_modes, group_modes, 0)
    kw_scale = jnp.stack([jnp.ones_like(kw_local), kw_local])[:, None, None, :, None, None]
    rows_all = rounded(spec * kw_scale).reshape(2, -1, 2 * block_size)
    rows_spec = rows_all[0]
    rows_grad = rows_all[1]

    def complex_matrix(weight):
        top = jnp.concatenate([weight[0], weight[1]], axis=1)
        bottom = jnp.concatenate([-weight[1], weight[0]], axis=1)
        return jnp.concatenate([top, bottom], axis=0)

    m1 = complex_matrix(w1)
    m2 = complex_matrix(w2)
    bias_first = jnp.concatenate([b1[0], b1[1]])
    bias_second = jnp.concatenate([b2[0], b2[1]])
    before = product(rows_spec, m1) + bias_first
    hidden = gelu_value(before).astype(jnp.bfloat16)
    filtered = (product(hidden, m2) + bias_second).astype(jnp.bfloat16)
    grad_hidden = adjoint(rows_grad, m2)
    grad_before = (grad_hidden * gelu_slope(before)).astype(jnp.bfloat16)
    grad_spec = adjoint(grad_before, m1).astype(jnp.bfloat16)

    def fold(full):
        return jnp.stack(
            [
                full[:block_size, :block_size] + full[block_size:, block_size:],
                full[:block_size, block_size:] - full[block_size:, :block_size],
            ]
        )

    second = fold(outer(hidden, rows_grad))
    first = fold(outer(rows_spec, grad_before))

    back_in = jnp.stack([filtered, grad_spec]).reshape(spec.shape)
    to_real = jnp.stack([cos_lead, cos_rest, sin_lead, sin_rest])
    to_imag = jnp.stack([-sin_lead, -sin_rest, cos_lead, cos_rest])
    inv_form = "qah,nsakc->qnshkc"
    back = jnp.einsum(inv_form, to_real, back_in[:, :, :, :, 0], preferred_element_type=jnp.float32) + jnp.einsum(
        inv_form, to_imag, back_in[:, :, :, :, 1], preferred_element_type=jnp.float32
    )
    back_real = back[0] + back[1]
    back_imag = back[2] + back[3]
    back_stack = jnp.stack([back_real[0], back_imag[0], back_real[1], back_imag[1]]).astype(jnp.bfloat16)
    moved = lax.all_to_all(back_stack, "llo", split_axis=4, concat_axis=3, tiled=True)
    back_real = moved[0::2]
    back_imag = moved[1::2]
    spatial = longitude_inverse(back_real[0], back_imag[0], wide_cosine, wide_sine, scale)
    grad_spatial = longitude_inverse(back_real[1], back_imag[1], lon_cosine, lon_sine, scale)
    out_stack = jnp.stack([spatial.astype(jnp.bfloat16), grad_spatial.astype(jnp.bfloat16)])
    out_tokens = lax.all_to_all(out_stack, LON, split_axis=3, concat_axis=4, tiled=True)
    share = blocks // member_count
    pieces = group * member_count
    weight_size = 2 * 2 * block_size * block_size
    weight_piece = weight_size // pieces
    payload = jnp.concatenate([first.reshape(-1), second.reshape(-1)]).reshape(
        group, member_count, weight_piece
    )
    payload = jnp.transpose(payload, (1, 0, 2)).reshape(pieces, weight_piece)
    payload, out_tokens = lax.optimization_barrier((payload, out_tokens))
    spatial_tokens = out_tokens[0]
    grad_field = out_tokens[1]

    mixed = (spatial_tokens.astype(jnp.float32) + normed.astype(jnp.float32)).astype(jnp.bfloat16)
    grad_normed = cot_field.astype(jnp.float32) + grad_field.astype(jnp.float32)
    gain_row = jnp.sum(grad_normed * standard, axis=(0, 1, 2))
    grad_hat = grad_normed * gain
    grad_in = inv_dev * (
        grad_hat
        - jnp.mean(grad_hat, axis=-1, keepdims=True)
        - standard * jnp.mean(grad_hat * standard, axis=-1, keepdims=True)
    )

    share = blocks // member_count
    gain_share = width // member_count
    row_factor = 1.0 / math.sqrt(member_count * samples * latitudes * modes)
    token_factor = 1.0 / math.sqrt(member_count * samples * latitudes * full_width)
    summed = jnp.sum(lax.all_to_all(payload, ("ens", "llo"), split_axis=0, concat_axis=0, tiled=True), axis=0)
    dest_member = jnp.arange(member_count * blocks)[:, None] // blocks
    keep = (dest_member == block // share).astype(jnp.float32)
    routed = lax.all_to_all(keep * summed[None, :], ("ens", "lhi"), split_axis=0, concat_axis=0, tiled=True)
    routed = routed.reshape(member_count, blocks, weight_piece)
    mine = lax.dynamic_slice_in_dim(routed, member * share, share, 1)
    local_result = mine.reshape(member_count, share * weight_piece)
    spread = jnp.broadcast_to(local_result[None], (group,) + local_result.shape)
    spread = lax.all_to_all(spread, "llo", split_axis=0, concat_axis=0, tiled=True)
    weights_all = spread.reshape(group, member_count, share, weight_piece)
    weights_all = jnp.transpose(weights_all, (2, 0, 1, 3)).reshape(share, 2, 2, block_size, block_size)
    sum_first = jnp.transpose(weights_all[:, 0], (1, 0, 2, 3))
    sum_second = jnp.transpose(weights_all[:, 1], (1, 0, 2, 3))

    devices = member_count * lon_count
    gain_rows = jnp.broadcast_to(
        gain_row.reshape(member_count, 1, gain_share), (member_count, devices // member_count, gain_share)
    ).reshape(devices, gain_share)
    gain_rows = lax.all_to_all(gain_rows, ("ens", "lhi", "llo"), split_axis=0, concat_axis=0, tiled=True)
    sum_gain = jnp.sum(gain_rows, axis=0)
    return (
        mixed[None],
        grad_in.astype(jnp.bfloat16)[None],
        sum_first * row_factor,
        sum_second * row_factor,
        sum_gain * token_factor,
    )


def solution(mesh):
    ens_size, lon_size = mesh.devices.shape
    view = Mesh(
        mesh.devices.reshape(ens_size, lon_size // GROUP, GROUP), ("ens", "lhi", "llo")
    )
    token_spec = P("ens", None, None, LON, None)
    return jax.shard_map(
        body,
        mesh=view,
        in_specs=(token_spec, token_spec, P(), P(), P(), P(), P()),
        out_specs=(
            token_spec,
            token_spec,
            P(None, "ens", None, None),
            P(None, "ens", None, None),
            P("ens"),
        ),
        check_vma=False,
    )
```

```python
import math

import jax
import jax.numpy as jnp
from jax import lax
from jax.sharding import Mesh
from jax.sharding import PartitionSpec as P

eps_norm = 1e-05
gelu_coef = 0.044715
GROUP = 8


def rounded(value):
    return lax.optimization_barrier(value.astype(jnp.bfloat16))


def gelu_value(value):
    factor = math.sqrt(2.0 / math.pi)
    return 0.5 * value * (1.0 + jnp.tanh(factor * (value + gelu_coef * value * value * value)))


def gelu_slope(value):
    factor = math.sqrt(2.0 / math.pi)
    tangent = jnp.tanh(factor * (value + gelu_coef * value * value * value))
    return 0.5 * (1.0 + tangent) + 0.5 * value * (1.0 - tangent * tangent) * factor * (
        1.0 + 3.0 * gelu_coef * value * value
    )


def table_parts(table):
    leading = table.astype(jnp.bfloat16)
    remainder = (table - leading.astype(jnp.float32)).astype(jnp.bfloat16)
    return (leading, remainder)


def data_table(form, data, parts):
    return jnp.einsum(form, data, parts[0], preferred_element_type=jnp.float32) + jnp.einsum(
        form, data, parts[1], preferred_element_type=jnp.float32
    )


def table_data(form, parts, data):
    return jnp.einsum(form, parts[0], data, preferred_element_type=jnp.float32) + jnp.einsum(
        form, parts[1], data, preferred_element_type=jnp.float32
    )


def longitude_tables(length, weights):
    places = jnp.arange(length, dtype=jnp.int32)
    numbers = jnp.arange(length // 2, dtype=jnp.int32)
    product = places[:, None] * numbers[None, :] % length
    angle = product.astype(jnp.float32) * (2.0 * math.pi / length)
    return (
        table_parts(jnp.cos(angle) * weights[None, :]),
        table_parts(jnp.sin(angle) * weights[None, :]),
    )


def latitude_tables(length):
    places = jnp.arange(length, dtype=jnp.int32)
    product = places[:, None] * places[None, :] % length
    angle = product.astype(jnp.float32) * (2.0 * math.pi / length)
    return (table_parts(jnp.cos(angle)), table_parts(jnp.sin(angle)))


def longitude_forward(field, cosine, sine, scale):
    real = data_table("nshwc,wk->nshkc", field, cosine) * scale
    imag = -data_table("nshwc,wk->nshkc", field, sine) * scale
    return (real, imag)


def longitude_inverse(real, imag, cosine, sine, scale):
    first = data_table("shkc,wk->shwc", real, cosine)
    second = data_table("shkc,wk->shwc", imag, sine)
    return (first - second) * scale


def latitude_forward(real, imag, cosine, sine):
    out_real = table_data("ah,nshkc->nsakc", cosine, real) + table_data("ah,nshkc->nsakc", sine, imag)
    out_imag = table_data("ah,nshkc->nsakc", cosine, imag) - table_data("ah,nshkc->nsakc", sine, real)
    return (out_real, out_imag)


def latitude_inverse(real, imag, cosine, sine):
    out_real = table_data("ah,nsakc->nshkc", cosine, real) - table_data("ah,nsakc->nshkc", sine, imag)
    out_imag = table_data("ah,nsakc->nshkc", cosine, imag) + table_data("ah,nsakc->nshkc", sine, real)
    return (out_real, out_imag)


def product(rows, weight):
    return jnp.dot(rows, weight, preferred_element_type=jnp.float32)


def adjoint(rows, weight):
    return lax.dot_general(rows, weight, (((1,), (1,)), ((), ())), preferred_element_type=jnp.float32)


def outer(left, right):
    return lax.dot_general(left, right, (((0,), (0,)), ((), ())), preferred_element_type=jnp.float32)


LON = ("lhi", "llo")


def body(tokens, cotangent, gain, weight_one, weight_two, bias_one, bias_two):
    field = tokens[0]
    cot_field = cotangent[0]
    samples, latitudes, local_width, width = field.shape
    lon_count = lax.axis_size(LON)
    group = lax.axis_size("llo")
    member_count = lax.axis_size("ens")
    full_width = local_width * lon_count
    modes = full_width // 2
    blocks = weight_one.shape[1]
    block_size = weight_one.shape[2]
    group_modes = modes // group
    block = lax.axis_index("lhi")
    member = lax.axis_index("ens")
    scale = 1.0 / math.sqrt(latitudes * full_width)
    full_weights = jnp.where(jnp.arange(modes) == 0, 1.0, 2.0).astype(jnp.float32)
    unit_weights = jnp.ones((modes,), jnp.float32)
    lon_cosine, lon_sine = longitude_tables(full_width, unit_weights)
    wide_cosine, wide_sine = longitude_tables(full_width, full_weights)
    lat_cosine, lat_sine = latitude_tables(latitudes)

    w1 = lax.dynamic_index_in_dim(weight_one, block, 1, keepdims=False)
    w2 = lax.dynamic_index_in_dim(weight_two, block, 1, keepdims=False)
    b1 = lax.dynamic_slice_in_dim(bias_one, block * block_size, block_size, 1)
    b2 = lax.dynamic_slice_in_dim(bias_two, block * block_size, block_size, 1)

    values = field.astype(jnp.float32)
    center = values - jnp.mean(values, axis=-1, keepdims=True)
    inv_dev = lax.rsqrt(jnp.mean(center * center, axis=-1, keepdims=True) + eps_norm)
    standard = center * inv_dev
    normed = (standard * gain).astype(jnp.bfloat16)

    both = jnp.stack([normed, cot_field])
    cols = lax.all_to_all(both, LON, split_axis=4, concat_axis=3, tiled=True)
    forward_table = jnp.concatenate([lon_cosine[0], lon_cosine[1], lon_sine[0], lon_sine[1]], axis=1)
    spectra = jnp.einsum("nshwc,wm->nshmc", cols, forward_table, preferred_element_type=jnp.float32)
    part_real = rounded((spectra[:, :, :, :modes] + spectra[:, :, :, modes : 2 * modes]) * scale)
    part_imag = rounded(-(spectra[:, :, :, 2 * modes : 3 * modes] + spectra[:, :, :, 3 * modes :]) * scale)
    exchanged = jnp.stack([part_real[0], part_imag[0], part_real[1], part_imag[1]])
    local = lax.all_to_all(exchanged, "llo", split_axis=3, concat_axis=4, tiled=True)
    local_shape = local.shape[1:]
    cos_lead, cos_rest = lat_cosine
    sin_lead, sin_rest = lat_sine
    from_real = jnp.stack([cos_lead, cos_rest, -sin_lead, -sin_rest])
    from_imag = jnp.stack([sin_lead, sin_rest, cos_lead, cos_rest])
    lat_form = "qah,nshkc->qnsakc"
    spec = jnp.einsum(lat_form, from_real, local[0::2], preferred_element_type=jnp.float32) + jnp.einsum(
        lat_form, from_imag, local[1::2], preferred_element_type=jnp.float32
    )
    spec = jnp.stack([spec[0] + spec[1], spec[2] + spec[3]], axis=-2)
    position = lax.axis_index("llo")
    kw_local = lax.dynamic_slice_in_dim(full_weights, position * group_modes, group_modes, 0)
    kw_scale = jnp.stack([jnp.ones_like(kw_local), kw_local])[:, None, None, :, None, None]
    rows_all = rounded(spec * kw_scale).reshape(2, -1, 2 * block_size)
    rows_spec = rows_all[0]
    rows_grad = rows_all[1]

    def complex_matrix(weight):
        top = jnp.concatenate([weight[0], weight[1]], axis=1)
        bottom = jnp.concatenate([-weight[1], weight[0]], axis=1)
        return jnp.concatenate([top, bottom], axis=0)

    m1 = complex_matrix(w1)
    m2 = complex_matrix(w2)
    bias_first = jnp.concatenate([b1[0], b1[1]])
    bias_second = jnp.concatenate([b2[0], b2[1]])
    before = product(rows_spec, m1) + bias_first
    hidden = gelu_value(before).astype(jnp.bfloat16)
    filtered = (product(hidden, m2) + bias_second).astype(jnp.bfloat16)
    grad_hidden = adjoint(rows_grad, m2)
    grad_before = (grad_hidden * gelu_slope(before)).astype(jnp.bfloat16)
    grad_spec = adjoint(grad_before, m1).astype(jnp.bfloat16)

    def fold(full):
        return jnp.stack(
            [
                full[:block_size, :block_size] + full[block_size:, block_size:],
                full[:block_size, block_size:] - full[block_size:, :block_size],
            ]
        )

    second = fold(outer(hidden, rows_grad))
    first = fold(outer(rows_spec, grad_before))

    back_in = jnp.stack([filtered, grad_spec]).reshape(spec.shape)
    to_real = jnp.stack([cos_lead, cos_rest, sin_lead, sin_rest])
    to_imag = jnp.stack([-sin_lead, -sin_rest, cos_lead, cos_rest])
    inv_form = "qah,nsakc->qnshkc"
    back = jnp.einsum(inv_form, to_real, back_in[:, :, :, :, 0], preferred_element_type=jnp.float32) + jnp.einsum(
        inv_form, to_imag, back_in[:, :, :, :, 1], preferred_element_type=jnp.float32
    )
    back_real = back[0] + back[1]
    back_imag = back[2] + back[3]
    back_stack = jnp.stack([back_real[0], back_imag[0], back_real[1], back_imag[1]]).astype(jnp.bfloat16)
    moved = lax.all_to_all(back_stack, "llo", split_axis=4, concat_axis=3, tiled=True)
    back_real = moved[0::2]
    back_imag = moved[1::2]
    spatial = longitude_inverse(back_real[0], back_imag[0], wide_cosine, wide_sine, scale)
    grad_spatial = longitude_inverse(back_real[1], back_imag[1], lon_cosine, lon_sine, scale)
    out_stack = jnp.stack([spatial.astype(jnp.bfloat16), grad_spatial.astype(jnp.bfloat16)])
    out_tokens = lax.all_to_all(out_stack, LON, split_axis=3, concat_axis=4, tiled=True)
    spatial_tokens = out_tokens[0]
    grad_field = out_tokens[1]

    mixed = (spatial_tokens.astype(jnp.float32) + normed.astype(jnp.float32)).astype(jnp.bfloat16)
    grad_normed = cot_field.astype(jnp.float32) + grad_field.astype(jnp.float32)
    gain_row = jnp.sum(grad_normed * standard, axis=(0, 1, 2))
    grad_hat = grad_normed * gain
    grad_in = inv_dev * (
        grad_hat
        - jnp.mean(grad_hat, axis=-1, keepdims=True)
        - standard * jnp.mean(grad_hat * standard, axis=-1, keepdims=True)
    )

    share = blocks // member_count
    gain_share = width // member_count
    row_factor = 1.0 / math.sqrt(member_count * samples * latitudes * modes)
    token_factor = 1.0 / math.sqrt(member_count * samples * latitudes * full_width)
    pieces = group * member_count
    weight_size = 2 * 2 * block_size * block_size
    weight_piece = weight_size // pieces
    gain_piece = width // pieces
    payload = jnp.concatenate(
        [
            jnp.concatenate([first.reshape(-1), second.reshape(-1)]).reshape(group, member_count, weight_piece),
            gain_row.reshape(group, member_count, gain_piece),
        ],
        axis=2,
    )
    payload = jnp.transpose(payload, (1, 0, 2)).reshape(pieces, weight_piece + gain_piece)
    summed = jnp.sum(lax.all_to_all(payload, ("ens", "llo"), split_axis=0, concat_axis=0, tiled=True), axis=0)
    dest_member = jnp.arange(member_count * blocks)[:, None] // blocks
    keep = (dest_member == block // share).astype(jnp.float32)
    routed = jnp.concatenate(
        [
            keep * summed[None, :weight_piece],
            jnp.broadcast_to(summed[None, weight_piece:], (member_count * blocks, gain_piece)),
        ],
        axis=1,
    )
    routed = lax.all_to_all(routed, ("ens", "lhi"), split_axis=0, concat_axis=0, tiled=True)
    routed = routed.reshape(member_count, blocks, weight_piece + gain_piece)
    mine = lax.dynamic_slice_in_dim(routed[:, :, :weight_piece], member * share, share, 1)
    gain_part = jnp.sum(routed[:, :, weight_piece:], axis=1)
    local_result = jnp.concatenate([mine.reshape(member_count, share * weight_piece), gain_part], axis=1)
    spread = jnp.broadcast_to(local_result[None], (group,) + local_result.shape)
    spread = lax.all_to_all(spread, "llo", split_axis=0, concat_axis=0, tiled=True)
    weights_all = spread[:, :, : share * weight_piece].reshape(group, member_count, share, weight_piece)
    weights_all = jnp.transpose(weights_all, (2, 0, 1, 3)).reshape(share, 2, 2, block_size, block_size)
    sum_first = jnp.transpose(weights_all[:, 0], (1, 0, 2, 3))
    sum_second = jnp.transpose(weights_all[:, 1], (1, 0, 2, 3))
    sum_gain = spread[:, :, share * weight_piece :].reshape(width)
    sum_gain = lax.dynamic_slice_in_dim(sum_gain, member * gain_share, gain_share, 0)
    return (
        mixed[None],
        grad_in.astype(jnp.bfloat16)[None],
        sum_first * row_factor,
        sum_second * row_factor,
        sum_gain * token_factor,
    )


def solution(mesh):
    ens_size, lon_size = mesh.devices.shape
    view = Mesh(
        mesh.devices.reshape(ens_size, lon_size // GROUP, GROUP), ("ens", "lhi", "llo")
    )
    token_spec = P("ens", None, None, LON, None)
    return jax.shard_map(
        body,
        mesh=view,
        in_specs=(token_spec, token_spec, P(), P(), P(), P(), P()),
        out_specs=(
            token_spec,
            token_spec,
            P(None, "ens", None, None),
            P(None, "ens", None, None),
            P("ens"),
        ),
        check_vma=False,
    )
```
